32 devices in a mesh: ctx: 4 (over y, core), ep: 8 (over z, x).
Axes of the slice: x: 2, y: 2, z: 4, core: 2. Of those that a mesh axis runs over, the one named last changes fastest.
Arguments:
- tokens: bfloat16 [1024, 3584], P('ep', 'ctx'), may hold values from -6 to 6
- cotangent: bfloat16 [1024, 3584], P('ep', 'ctx'), may hold values from -0.8984375 to 0.8984375
- expert_ids: int32 [1024, 1], P('ep'), may hold values from 0 to 7; in each aligned block of 128 rows (0 to 127, 128 to 255, ...) at most 24 rows name the same one
- route_gates: float32 [1024, 1], P('ep'), may hold values from 0.1 to 1
- w_gate: bfloat16 [8, 3584, 2048], P('ep', None, 'ctx'), may hold values from -0.125 to 0.125
- w_up: bfloat16 [8, 3584, 2048], P('ep', None, 'ctx'), may hold values from -0.09375 to 0.09375
- w_down: bfloat16 [8, 2048, 3584], P('ep', 'ctx'), may hold values from -0.1875 to 0.1875
Outputs:
- layer_out: bfloat16 [1024, 3584], P('ep', 'ctx')
- input_grad: bfloat16 [1024, 3584], P('ep', 'ctx')
- gate_grad: float32 [1024, 1], P('ep')
- w_gate_grad: bfloat16 [8, 3584, 2048], P('ep', None, 'ctx')
- w_up_grad: bfloat16 [8, 3584, 2048], P('ep', None, 'ctx')
The draws below stay inside these ranges and needn't reach their ends.
Inputs may be any that keep to these rules, and one draw needn't show every extreme that they name: `expert_ids`: within each aligned block of 128 tokens (the tokens of one index of ep) no expert is named more than 24 times, a bound that some block reaches; the routes of one token name different experts.
All inputs are finite; a program needn't handle non-finite values.
Results may differ from the reference program's by a relative error of at most 0.015.
Values may be sent and summed in bfloat16 or wider, within the bound.
No kernel may reach another device: no remote copies, remote signals or barrier semaphores. Data moves between devices by JAX's collectives and lax.ppermute only.
A program may use at most 128 MiB of HBM per device.

```python
import math
import jax
import jax.numpy as jnp
import numpy as np
from jax import lax

D = 3584
FF = 2048
ROUTES = 1
TOK_DEV = 128
EXPERTS = 8
TOKENS = 1024
CAP = 24
N_CTX = 4
N_EP = 8


def with_spikes(array, own_key, source, target, shards_of, factor):
    def block_of(dim):
        return (jnp.arange(array.shape[dim]) // (array.shape[dim] // shards_of)).reshape((-1,) + (1,) * (array.ndim - 1 - dim))

    first = jax.random.permutation(own_key, shards_of)[block_of(target)]
    second = (block_of(target) + shards_of // 2) % shards_of
    return jnp.where((block_of(source) == first) | (block_of(source) == second), factor * array, array)


def level_of(key, extent, pieces, smallest, high):
    def one(dim, blocks):
        draws = jax.random.uniform(jax.random.fold_in(jax.random.fold_in(key, 6), dim), (blocks,), jnp.float32, smallest / len(pieces), high / len(pieces))
        return jnp.repeat(jnp.exp(draws), extent[dim] // blocks).reshape((-1,) + (1,) * (len(extent) - dim - 1))

    level = one(*pieces[0])
    for cut in pieces[1:]:
        level = level * one(*cut)
    return level


def shared_out(key, own, number, rows, number_of, top, most, slope):
    order = jax.random.permutation(key, number_of)
    heavy_load, common = load_shares(number_of, rows * top, most, slope, True), load_shares(number_of, rows * top, most, slope, False)
    places = jnp.arange(number_of)

    def named(sizes, rotation):
        used = int((sizes > 0).sum())
        fixed = max(1, used // 4)
        passed = fixed + (places - fixed + rotation * (used - fixed)) % max(1, number_of - fixed)
        return jnp.zeros((number_of,), jnp.int32).at[order[jnp.where(places < fixed, places, passed)]].set(jnp.asarray(sizes, jnp.int32))

    sizes = jnp.where(number % 4 == 0, named(heavy_load, number // 4), named(common, number - number // 4 - 1))
    mixed = jax.random.permutation(jax.random.fold_in(own, 3), number_of)
    source_of, sink = mixed[0:number_of // 2 * 2:2], mixed[1:number_of // 2 * 2:2]
    slack = jnp.minimum(sizes[source_of] - 1, most - sizes[sink]) // 2
    slack = jnp.where((source_of == order[0]) | (sink == order[0]) | (sizes[sink] == 0), 0, jnp.maximum(slack, 0))
    passed = jax.random.randint(jax.random.fold_in(own, 4), (number_of // 2,), 0, 1 << 20) % (slack + 1)
    sizes = sizes.at[source_of].add(-passed).at[sink].add(passed)
    items = jnp.searchsorted(jnp.cumsum(sizes), jnp.arange(rows * top), side="right").astype(jnp.int32)
    grid = items.reshape(top, rows).T
    grid = grid[jax.random.permutation(jax.random.fold_in(own, 1), rows)]
    rotation = jax.random.randint(jax.random.fold_in(own, 2), (rows, 1), 0, top)
    return jnp.take_along_axis(grid, (jnp.arange(top)[None, :] + rotation) % top, axis=1)


def load_shares(amount, total, limit, lean, full):
    portions = [(1 << 20) // math.isqrt(grade ** lean) + 1 for grade in range(1, amount + 1)]
    largest = limit if full else min(limit, max(-(-total // amount), total * portions[0] // sum(portions)))
    least = 1 if total - largest >= amount - 1 else 0
    holding, spare = [largest] + [least] * (amount - 1), total - largest - least * (amount - 1)
    while spare > 0:
        free = [i for i in range(1, amount) if holding[i] < largest] or [i for i in range(1, amount) if holding[i] < limit]
        pool, left = sum([portions[i] for i in free]), spare
        for i in free:
            extra = min(limit - holding[i], max(1, left * portions[i] // pool), spare)
            holding[i] = holding[i] + extra
            spare = spare - extra
    return np.array(holding)


def scatter_about(key, extent, width, most, shards=(), held_as=jnp.bfloat16):
    drawn = width * jax.random.normal(key, extent, jnp.float32)
    if shards:
        drawn = drawn * level_of(key, extent, shards, -0.22, 0.18)
    return jnp.clip(drawn, -most, most).astype(held_as)


def noise_with(stream_key, extent, scale, reach, shards, heavy, kind=jnp.bfloat16):
    result = scale * jax.random.normal(stream_key, extent, jnp.float32)
    if shards:
        result = result * level_of(stream_key, extent, shards, -0.22, 0.18)
    return jnp.clip(with_spikes(result, jax.random.fold_in(stream_key, 3), *heavy), -reach, reach).astype(kind)


def setup_inputs(seed: int = 0) -> dict:
    key_of = jax.random.split(jax.random.key(seed), 8)
    tokens = scatter_about(key_of[0], (TOKENS, D), 1.0, 6.0, ((0, 8), (1, 4)))
    cotangent = scatter_about(key_of[1], (TOKENS, D), 0.15, 0.8984375, ((0, 8), (1, 4)))
    expert_ids_keys = jax.random.split(jax.random.fold_in(key_of[2], 1), TOKENS // TOK_DEV)
    expert_ids_turns = jax.random.permutation(jax.random.fold_in(key_of[2], 3), TOKENS // TOK_DEV)
    expert_ids = jax.vmap(lambda own, number: shared_out(jax.random.fold_in(key_of[2], 2), own, number, TOK_DEV, EXPERTS, ROUTES, CAP, 2))(expert_ids_keys, expert_ids_turns).reshape((TOKENS, ROUTES))
    route_gates = jnp.clip(0.1 + 0.9 * jax.random.uniform(key_of[3], (TOKENS, ROUTES), jnp.float32) ** level_of(key_of[3], (TOKENS, ROUTES), ((0, 8),), -0.2, 0.2), 0.1, 1.0)
    w_gate = noise_with(key_of[4], (EXPERTS, D, FF), D ** -0.5, 0.125, ((0, 8), (2, 4)), (2, 1, 4, 2.0))
    w_up = scatter_about(key_of[5], (EXPERTS, D, FF), D ** -0.5, 0.09375, ((0, 8), (2, 4)))
    w_down = noise_with(key_of[6], (EXPERTS, FF, D), FF ** -0.5, 0.1875, ((0, 8), (1, 4)), (1, 2, 4, 2.0))
    return {"tokens": tokens, "cotangent": cotangent, "expert_ids": expert_ids, "route_gates": route_gates, "w_gate": w_gate, "w_up": w_up, "w_down": w_down}


def reference(tokens, cotangent, expert_ids, route_gates, w_gate, w_up, w_down):
    group = FF // N_CTX
    slots = N_EP * CAP
    labels = jnp.arange(EXPERTS, dtype=jnp.int32)
    blocked = expert_ids.reshape(N_EP, TOK_DEV * ROUTES)
    onehot = (blocked[:, :, None] == labels[None, None, :]).astype(jnp.int32)
    earlier = (jnp.cumsum(onehot, axis=1) - onehot).astype(jnp.int32)
    slot_rank = jnp.sum(earlier * onehot, axis=2).astype(jnp.int32)
    source = jnp.arange(N_EP, dtype=jnp.int32)[:, None]
    position = (source * CAP + slot_rank).reshape(TOKENS, ROUTES).astype(jnp.int32)
    owner = jnp.broadcast_to(jnp.arange(TOKENS, dtype=jnp.int32)[:, None], (TOKENS, ROUTES))
    table = jnp.full((EXPERTS, slots), TOKENS, jnp.int32).at[expert_ids, position].set(owner)
    slot_gates = jnp.zeros((EXPERTS, slots), jnp.float32).at[expert_ids, position].set(route_gates.astype(jnp.float32))
    padded_x = jnp.concatenate([tokens, jnp.zeros((1, D), tokens.dtype)], axis=0)
    padded_dy = jnp.concatenate([cotangent, jnp.zeros((1, D), cotangent.dtype)], axis=0)

    def one_expert(operands):
        gate_w, up_w, down_w, rows, gates = operands
        rows_in = padded_x[rows]
        grads_in = padded_dy[rows]
        pre_gate = jnp.dot(rows_in, gate_w, preferred_element_type=jnp.float32)
        pre_up = jnp.dot(rows_in, up_w, preferred_element_type=jnp.float32)
        sigma = jax.nn.sigmoid(pre_gate)
        activated = pre_gate * sigma
        hidden = (activated * pre_up).astype(jnp.bfloat16)
        hidden3 = hidden.astype(jnp.float32).reshape(slots, N_CTX, group)
        down3 = down_w.astype(jnp.float32).reshape(N_CTX, group, D)
        terms = jnp.einsum("snf,nfd->nsd", hidden3, down3, precision=lax.Precision.HIGHEST)
        rounded = lax.optimization_barrier(terms.astype(jnp.bfloat16))
        expert_out = jnp.sum(rounded.astype(jnp.float32), axis=0).astype(jnp.bfloat16)
        hidden_grad = gates[:, None] * jnp.dot(grads_in, down_w.T, preferred_element_type=jnp.float32)
        grad_gate = (hidden_grad * pre_up * sigma * (1.0 + pre_gate * (1.0 - sigma))).astype(jnp.bfloat16)
        grad_up = (hidden_grad * activated).astype(jnp.bfloat16)
        gate3 = grad_gate.astype(jnp.float32).reshape(slots, N_CTX, group)
        up3 = grad_up.astype(jnp.float32).reshape(slots, N_CTX, group)
        gate_w3 = gate_w.astype(jnp.float32).reshape(D, N_CTX, group)
        up_w3 = up_w.astype(jnp.float32).reshape(D, N_CTX, group)
        back = jnp.einsum("snf,dnf->nsd", gate3, gate_w3, precision=lax.Precision.HIGHEST)
        back = back + jnp.einsum("snf,dnf->nsd", up3, up_w3, precision=lax.Precision.HIGHEST)
        back_rounded = lax.optimization_barrier(back.astype(jnp.bfloat16))
        slot_grad = jnp.sum(back_rounded.astype(jnp.float32), axis=0).astype(jnp.bfloat16)
        gate_w_grad = jnp.dot(rows_in.T, grad_gate, preferred_element_type=jnp.float32).astype(jnp.bfloat16)
        up_w_grad = jnp.dot(rows_in.T, grad_up, preferred_element_type=jnp.float32).astype(jnp.bfloat16)
        return expert_out, slot_grad, gate_w_grad, up_w_grad

    expert_out, slot_grad, gate_w_grad, up_w_grad = lax.map(one_expert, (w_gate, w_up, w_down, table, slot_gates))
    picked = expert_out[expert_ids, position].astype(jnp.float32)
    layer_out = jnp.sum(route_gates.astype(jnp.float32)[:, :, None] * picked, axis=1).astype(jnp.bfloat16)
    gate_grad = jnp.sum(picked * cotangent.astype(jnp.float32)[:, None, :], axis=2)
    input_grad = jnp.sum(slot_grad[expert_ids, position].astype(jnp.float32), axis=1).astype(jnp.bfloat16)
    return layer_out, input_grad, gate_grad, gate_w_grad, up_w_grad
```

```python
import jax
import jax.numpy as jnp
from jax import lax
from jax.sharding import PartitionSpec as P


def route_onehot(expert_ids, experts, capacity):
    tok_rows, routes = expert_ids.shape
    flat_ids = expert_ids.reshape(-1)
    labels = jnp.arange(experts, dtype=jnp.int32)
    onehot = (flat_ids[:, None] == labels[None, :]).astype(jnp.int32)
    earlier = jnp.cumsum(onehot, axis=0) - onehot
    slot_rank = jnp.sum(earlier * onehot, axis=1)
    slot_ids = (flat_ids * capacity + slot_rank).reshape(tok_rows, routes)
    positions = jnp.arange(experts * capacity, dtype=jnp.int32)
    return [slot_ids[:, r][:, None] == positions[None, :] for r in range(routes)]


def split_f32(values):
    hi = values.astype(jnp.bfloat16)
    lo = (values - hi.astype(jnp.float32)).astype(jnp.bfloat16)
    return hi, lo


def join_f32(hi, lo):
    return hi.astype(jnp.float32) + lo.astype(jnp.float32)


def ctx_bits(n_ctx):
    bits = n_ctx.bit_length() - 1
    assert 1 << bits == n_ctx
    return bits


def xor_pairs(n_ctx, bit):
    return [(i, i ^ (1 << bit)) for i in range(n_ctx)]


def gather_blocks(block, n_ctx, me):
    held = block[None]
    for bit in reversed(range(ctx_bits(n_ctx))):
        other = lax.ppermute(held, "ctx", xor_pairs(n_ctx, bit))
        mine_first = ((me >> bit) & 1) == 0
        pair = jnp.where(
            mine_first, jnp.stack([held, other], axis=1), jnp.stack([other, held], axis=1)
        )
        held = pair.reshape((-1,) + block.shape)
    return held


def scatter_sum(blocks, n_ctx, me):
    acc = blocks
    for bit in range(ctx_bits(n_ctx)):
        halves = acc.reshape((-1, 2) + acc.shape[1:])
        keep_first = ((me >> bit) & 1) == 0
        keep = jnp.where(keep_first, halves[:, 0], halves[:, 1])
        send = jnp.where(keep_first, halves[:, 1], halves[:, 0]).astype(jnp.bfloat16)
        got = lax.ppermute(send, "ctx", xor_pairs(n_ctx, bit))
        acc = keep + got.astype(jnp.float32)
    return acc[0]


def shards(tokens, cotangent, expert_ids, route_gates, w_gate, w_up, w_down):
    tok_rows, routes = expert_ids.shape
    experts = lax.axis_size("ep")
    n_ctx = lax.axis_size("ctx")
    me = lax.axis_index("ctx")
    capacity = 3 * tok_rows * routes // (2 * experts)
    slot_count = experts * capacity
    col_width = tokens.shape[1]
    pad = 128
    route_maps = route_onehot(expert_ids, experts, capacity)

    slot_gates = jnp.zeros((slot_count,), jnp.float32)
    placed = jnp.zeros((slot_count, 2 * col_width), jnp.float32)
    both = jnp.concatenate([tokens, cotangent], axis=1)
    for r, chosen in enumerate(route_maps):
        slot_gates = slot_gates + jnp.sum(jnp.where(chosen, route_gates[:, r][:, None], 0.0), axis=0)
        placed = placed + jnp.einsum(
            "ts,tc->sc", chosen.astype(jnp.bfloat16), both, preferred_element_type=jnp.float32
        )
    gate_hi, gate_lo = split_f32(slot_gates)
    gate_cols = jnp.zeros((slot_count, pad), jnp.bfloat16)
    gate_cols = gate_cols.at[:, 0].set(gate_hi).at[:, 1].set(gate_lo)
    sent = jnp.concatenate([placed.astype(jnp.bfloat16), gate_cols], axis=1)
    sent = sent.reshape(experts, capacity, 2 * col_width + pad)
    got = lax.all_to_all(sent, "ep", split_axis=0, concat_axis=0, tiled=True)
    got = got.reshape(slot_count, 2 * col_width + pad)
    gate_column = join_f32(got[:, 2 * col_width], got[:, 2 * col_width + 1])[:, None]

    full = gather_blocks(got[:, : 2 * col_width], n_ctx, me)
    rows_in = full[:, :, :col_width]
    grads_in = full[:, :, col_width:]

    group = w_gate.shape[2]
    gate_w = w_gate[0].reshape(n_ctx, col_width, group)
    up_w = w_up[0].reshape(n_ctx, col_width, group)
    down_w = w_down[0].reshape(group, n_ctx, col_width)

    pre_gate = jnp.einsum("nsd,ndf->sf", rows_in, gate_w, preferred_element_type=jnp.float32)
    pre_up = jnp.einsum("nsd,ndf->sf", rows_in, up_w, preferred_element_type=jnp.float32)
    sigma = jax.nn.sigmoid(pre_gate)
    activated = pre_gate * sigma
    hidden = (activated * pre_up).astype(jnp.bfloat16)
    partial_out = jnp.einsum(
        "sf,fnd->nsd", hidden, down_w, preferred_element_type=jnp.float32
    ).astype(jnp.bfloat16)
    gate_part = jnp.einsum(
        "nsd,nsd->s", partial_out.astype(jnp.float32), grads_in.astype(jnp.float32)
    )
    gate_sum = lax.psum(gate_part, "ctx")
    expert_out = scatter_sum(partial_out.astype(jnp.float32), n_ctx, me).astype(jnp.bfloat16)

    hidden_grad = gate_column * jnp.einsum(
        "nsd,fnd->sf", grads_in, down_w, preferred_element_type=jnp.float32
    )
    grad_gate = (hidden_grad * pre_up * sigma * (1.0 + pre_gate * (1.0 - sigma))).astype(
        jnp.bfloat16
    )
    grad_up = (hidden_grad * activated).astype(jnp.bfloat16)
    back_terms = jnp.einsum(
        "sf,ndf->nsd", grad_gate, gate_w, preferred_element_type=jnp.float32
    ) + jnp.einsum("sf,ndf->nsd", grad_up, up_w, preferred_element_type=jnp.float32)
    back_terms = back_terms.astype(jnp.bfloat16).astype(jnp.float32)
    slot_grad = scatter_sum(back_terms, n_ctx, me).astype(jnp.bfloat16)

    w_gate_grad = jnp.einsum(
        "nsd,sf->ndf", rows_in, grad_gate, preferred_element_type=jnp.float32
    ).astype(jnp.bfloat16).reshape(1, n_ctx * col_width, group)
    w_up_grad = jnp.einsum(
        "nsd,sf->ndf", rows_in, grad_up, preferred_element_type=jnp.float32
    ).astype(jnp.bfloat16).reshape(1, n_ctx * col_width, group)

    gg_hi, gg_lo = split_f32(gate_sum)
    gg_cols = jnp.zeros((slot_count, pad), jnp.bfloat16)
    gg_cols = gg_cols.at[:, 0].set(gg_hi).at[:, 1].set(gg_lo)
    back = jnp.concatenate([expert_out, slot_grad, gg_cols], axis=1)
    back = back.reshape(experts, capacity, 2 * col_width + pad)
    back = lax.all_to_all(back, "ep", split_axis=0, concat_axis=0, tiled=True)
    back = back.reshape(slot_count, 2 * col_width + pad)
    slot_gg = join_f32(back[:, 2 * col_width], back[:, 2 * col_width + 1])

    picked = jnp.zeros((tok_rows, 2 * col_width), jnp.float32)
    layer_out = jnp.zeros((tok_rows, col_width), jnp.float32)
    gate_terms = []
    for r, chosen in enumerate(route_maps):
        rows_r = jnp.dot(
            chosen.astype(jnp.bfloat16), back[:, : 2 * col_width], preferred_element_type=jnp.float32
        )
        layer_out = layer_out + route_gates[:, r][:, None] * rows_r[:, :col_width]
        picked = picked + rows_r
        gate_terms.append(jnp.sum(jnp.where(chosen, slot_gg[None, :], 0.0), axis=1))
    input_grad = picked[:, col_width:]
    gate_grad = jnp.stack(gate_terms, axis=1)
    return (
        layer_out.astype(jnp.bfloat16),
        input_grad.astype(jnp.bfloat16),
        gate_grad,
        w_gate_grad,
        w_up_grad,
    )


def solution(mesh):
    in_specs = (
        P("ep", "ctx"),
        P("ep", "ctx"),
        P("ep", None),
        P("ep", None),
        P("ep", None, "ctx"),
        P("ep", None, "ctx"),
        P("ep", "ctx", None),
    )
    out_specs = (
        P("ep", "ctx"),
        P("ep", "ctx"),
        P("ep", None),
        P("ep", None, "ctx"),
        P("ep", None, "ctx"),
    )
    return jax.shard_map(shards, mesh=mesh, in_specs=in_specs, out_specs=out_specs, check_vma=False)
```

```python
import jax
import jax.numpy as jnp
from jax import lax
from jax.sharding import PartitionSpec as P


def route_onehot(expert_ids, experts, capacity):
    tok_rows, routes = expert_ids.shape
    flat_ids = expert_ids.reshape(-1)
    labels = jnp.arange(experts, dtype=jnp.int32)
    onehot = (flat_ids[:, None] == labels[None, :]).astype(jnp.int32)
    earlier = jnp.cumsum(onehot, axis=0) - onehot
    slot_rank = jnp.sum(earlier * onehot, axis=1)
    slot_ids = (flat_ids * capacity + slot_rank).reshape(tok_rows, routes)
    positions = jnp.arange(experts * capacity, dtype=jnp.int32)
    return [slot_ids[:, r][:, None] == positions[None, :] for r in range(routes)]


def split_f32(values):
    hi = values.astype(jnp.bfloat16)
    lo = (values - hi.astype(jnp.float32)).astype(jnp.bfloat16)
    return hi, lo


def join_f32(hi, lo):
    return hi.astype(jnp.float32) + lo.astype(jnp.float32)


def ctx_bits(n_ctx):
    bits = n_ctx.bit_length() - 1
    assert 1 << bits == n_ctx
    return bits


def xor_pairs(n_ctx, bit):
    return [(i, i ^ (1 << bit)) for i in range(n_ctx)]


def gather_blocks(block, n_ctx, me):
    held = block[None]
    for bit in reversed(range(ctx_bits(n_ctx))):
        other = lax.ppermute(held, "ctx", xor_pairs(n_ctx, bit))
        mine_first = ((me >> bit) & 1) == 0
        pair = jnp.where(
            mine_first, jnp.stack([held, other], axis=1), jnp.stack([other, held], axis=1)
        )
        held = pair.reshape((-1,) + block.shape)
    return held


def scatter_sum(blocks, n_ctx, me):
    acc = blocks
    for bit in range(ctx_bits(n_ctx)):
        halves = acc.reshape((-1, 2) + acc.shape[1:])
        keep_first = ((me >> bit) & 1) == 0
        keep = jnp.where(keep_first, halves[:, 0], halves[:, 1])
        send = jnp.where(keep_first, halves[:, 1], halves[:, 0]).astype(jnp.bfloat16)
        got = lax.ppermute(send, "ctx", xor_pairs(n_ctx, bit))
        acc = keep + got.astype(jnp.float32)
    return acc[0]


def all_sum(values, n_ctx):
    for bit in range(ctx_bits(n_ctx)):
        values = values + lax.ppermute(values, "ctx", xor_pairs(n_ctx, bit))
    return values


def with_cols(rows, values, pad):
    hi, lo = split_f32(values)
    cols = jnp.zeros((rows.shape[0], pad), jnp.bfloat16)
    cols = cols.at[:, 0].set(hi).at[:, 1].set(lo)
    return jnp.concatenate([rows, cols], axis=1)


def shards(tokens, cotangent, expert_ids, route_gates, w_gate, w_up, w_down):
    tok_rows, routes = expert_ids.shape
    experts = lax.axis_size("ep")
    n_ctx = lax.axis_size("ctx")
    me = lax.axis_index("ctx")
    capacity = 3 * tok_rows * routes // (2 * experts)
    slot_count = experts * capacity
    col_width = tokens.shape[1]
    pad = 128
    route_maps = route_onehot(expert_ids, experts, capacity)

    def place(values):
        placed = jnp.zeros((slot_count, values.shape[1]), jnp.float32)
        for chosen in route_maps:
            placed = placed + jnp.einsum(
                "ts,tc->sc", chosen.astype(jnp.bfloat16), values, preferred_element_type=jnp.float32
            )
        return placed.astype(jnp.bfloat16)

    def to_experts(rows):
        sent = rows.reshape(experts, capacity, rows.shape[1])
        got = lax.all_to_all(sent, "ep", split_axis=0, concat_axis=0, tiled=True)
        return got.reshape(slot_count, rows.shape[1])

    slot_gates = jnp.zeros((slot_count,), jnp.float32)
    for r, chosen in enumerate(route_maps):
        slot_gates = slot_gates + jnp.sum(jnp.where(chosen, route_gates[:, r][:, None], 0.0), axis=0)
    got_x = to_experts(with_cols(place(tokens), slot_gates, pad))
    gate_column = join_f32(got_x[:, col_width], got_x[:, col_width + 1])[:, None]
    rows_in = gather_blocks(got_x[:, :col_width], n_ctx, me)
    got_dy = to_experts(place(cotangent))
    grads_in = gather_blocks(got_dy, n_ctx, me)

    group = w_gate.shape[2]
    gate_w = w_gate[0].reshape(n_ctx, col_width, group)
    up_w = w_up[0].reshape(n_ctx, col_width, group)
    down_w = w_down[0]
    down_cols = [down_w[:, q * col_width : (q + 1) * col_width] for q in range(n_ctx)]

    pre_gate = jnp.einsum("nsd,ndf->sf", rows_in, gate_w, preferred_element_type=jnp.float32)
    pre_up = jnp.einsum("nsd,ndf->sf", rows_in, up_w, preferred_element_type=jnp.float32)
    sigma = jax.nn.sigmoid(pre_gate)
    activated = pre_gate * sigma
    hidden = (activated * pre_up).astype(jnp.bfloat16)
    partial_out = jnp.stack(
        [jnp.dot(hidden, cols, preferred_element_type=jnp.float32) for cols in down_cols]
    ).astype(jnp.bfloat16)
    gate_part = jnp.einsum(
        "nsd,nsd->s", partial_out.astype(jnp.float32), grads_in.astype(jnp.float32)
    )
    expert_out = scatter_sum(partial_out.astype(jnp.float32), n_ctx, me).astype(jnp.bfloat16)
    gate_sum = all_sum(gate_part, n_ctx)
    back_out = to_experts(with_cols(expert_out, gate_sum, pad))

    contract_last = (((1,), (1,)), ((), ()))
    down_t = sum(
        lax.dot_general(grads_in[q], down_cols[q], contract_last, preferred_element_type=jnp.float32)
        for q in range(n_ctx)
    )
    hidden_grad = gate_column * down_t
    grad_gate = (hidden_grad * pre_up * sigma * (1.0 + pre_gate * (1.0 - sigma))).astype(
        jnp.bfloat16
    )
    grad_up = (hidden_grad * activated).astype(jnp.bfloat16)
    back_terms = jnp.einsum(
        "sf,ndf->nsd", grad_gate, gate_w, preferred_element_type=jnp.float32
    ) + jnp.einsum("sf,ndf->nsd", grad_up, up_w, preferred_element_type=jnp.float32)
    back_terms = back_terms.astype(jnp.bfloat16).astype(jnp.float32)
    slot_grad = scatter_sum(back_terms, n_ctx, me).astype(jnp.bfloat16)
    back_grad = to_experts(slot_grad)

    w_gate_grad = jnp.einsum(
        "nsd,sf->ndf", rows_in, grad_gate, preferred_element_type=jnp.float32
    ).astype(jnp.bfloat16).reshape(1, n_ctx * col_width, group)
    w_up_grad = jnp.einsum(
        "nsd,sf->ndf", rows_in, grad_up, preferred_element_type=jnp.float32
    ).astype(jnp.bfloat16).reshape(1, n_ctx * col_width, group)

    slot_gg = join_f32(back_out[:, col_width], back_out[:, col_width + 1])
    out_rows = back_out[:, :col_width]
    layer_out = jnp.zeros((tok_rows, col_width), jnp.float32)
    input_grad = jnp.zeros((tok_rows, col_width), jnp.float32)
    gate_terms = []
    for r, chosen in enumerate(route_maps):
        pick = chosen.astype(jnp.bfloat16)
        rows_r = jnp.dot(pick, out_rows, preferred_element_type=jnp.float32)
        layer_out = layer_out + route_gates[:, r][:, None] * rows_r
        input_grad = input_grad + jnp.dot(pick, back_grad, preferred_element_type=jnp.float32)
        gate_terms.append(jnp.sum(jnp.where(chosen, slot_gg[None, :], 0.0), axis=1))
    gate_grad = jnp.stack(gate_terms, axis=1)
    return (
        layer_out.astype(jnp.bfloat16),
        input_grad.astype(jnp.bfloat16),
        gate_grad,
        w_gate_grad,
        w_up_grad,
    )


def solution(mesh):
    in_specs = (
        P("ep", "ctx"),
        P("ep", "ctx"),
        P("ep", None),
        P("ep", None),
        P("ep", None, "ctx"),
        P("ep", None, "ctx"),
        P("ep", "ctx", None),
    )
    out_specs = (
        P("ep", "ctx"),
        P("ep", "ctx"),
        P("ep", None),
        P("ep", None, "ctx"),
        P("ep", None, "ctx"),
    )
    return jax.shard_map(shards, mesh=mesh, in_specs=in_specs, out_specs=out_specs, check_vma=False)
```

```python
import jax
import jax.numpy as jnp
from jax import lax
from jax.sharding import PartitionSpec as P


def route_onehot(expert_ids, experts, capacity, me_ep):
    tok_rows, routes = expert_ids.shape
    flat_ids = expert_ids.reshape(-1)
    labels = jnp.arange(experts, dtype=jnp.int32)
    onehot = (flat_ids[:, None] == labels[None, :]).astype(jnp.int32)
    earlier = jnp.cumsum(onehot, axis=0) - onehot
    slot_rank = jnp.sum(earlier * onehot, axis=1)
    shift = (flat_ids - me_ep) % experts
    slot_ids = (shift * capacity + slot_rank).reshape(tok_rows, routes)
    positions = jnp.arange(experts * capacity, dtype=jnp.int32)
    return [slot_ids[:, r][:, None] == positions[None, :] for r in range(routes)]


def split_f32(values):
    hi = values.astype(jnp.bfloat16)
    lo = (values - hi.astype(jnp.float32)).astype(jnp.bfloat16)
    return hi, lo


def join_f32(hi, lo):
    return hi.astype(jnp.float32) + lo.astype(jnp.float32)


def ctx_bits(n_ctx):
    bits = n_ctx.bit_length() - 1
    assert 1 << bits == n_ctx
    return bits


def xor_pairs(n_ctx, bit):
    return [(i, i ^ (1 << bit)) for i in range(n_ctx)]


def gather_blocks(block, n_ctx, me):
    held = block[None]
    for bit in reversed(range(ctx_bits(n_ctx))):
        other = lax.ppermute(held, "ctx", xor_pairs(n_ctx, bit))
        mine_first = ((me >> bit) & 1) == 0
        pair = jnp.where(
            mine_first, jnp.stack([held, other], axis=1), jnp.stack([other, held], axis=1)
        )
        held = pair.reshape((-1,) + block.shape)
    return held


def scatter_sum(blocks, n_ctx, me):
    acc = blocks
    for bit in range(ctx_bits(n_ctx)):
        halves = acc.reshape((-1, 2) + acc.shape[1:])
        keep_first = ((me >> bit) & 1) == 0
        keep = jnp.where(keep_first, halves[:, 0], halves[:, 1])
        send = jnp.where(keep_first, halves[:, 1], halves[:, 0]).astype(jnp.bfloat16)
        got = lax.ppermute(send, "ctx", xor_pairs(n_ctx, bit))
        acc = keep + got.astype(jnp.float32)
    return acc[0]


def all_sum(values, n_ctx):
    for bit in range(ctx_bits(n_ctx)):
        values = values + lax.ppermute(values, "ctx", xor_pairs(n_ctx, bit))
    return values


def with_cols(rows, values, pad):
    hi, lo = split_f32(values)
    zeros = jnp.zeros((rows.shape[0], pad - 2), jnp.bfloat16)
    return jnp.concatenate([rows, hi[:, None], lo[:, None], zeros], axis=1)


def shards(tokens, cotangent, expert_ids, route_gates, w_gate, w_up, w_down):
    tok_rows, routes = expert_ids.shape
    experts = lax.axis_size("ep")
    n_ctx = lax.axis_size("ctx")
    me = lax.axis_index("ctx")
    capacity = 3 * tok_rows * routes // (2 * experts)
    slot_count = experts * capacity
    col_width = tokens.shape[1]
    pad = 128
    me_ep = lax.axis_index("ep")
    route_maps = route_onehot(expert_ids, experts, capacity, me_ep)

    def place(values):
        placed = jnp.zeros((slot_count, values.shape[1]), jnp.float32)
        for chosen in route_maps:
            placed = placed + jnp.einsum(
                "ts,tc->sc", chosen.astype(jnp.bfloat16), values, preferred_element_type=jnp.float32
            )
        return placed.astype(jnp.bfloat16)

    def exchange(rows, sign):
        blocks = rows.reshape(experts, capacity, rows.shape[1])
        moved = [blocks[0]]
        for s in range(1, experts):
            pairs = [(j, (j + sign * s) % experts) for j in range(experts)]
            moved.append(lax.ppermute(blocks[s], "ep", pairs))
        return jnp.stack(moved).reshape(slot_count, rows.shape[1])

    def to_experts(rows):
        return exchange(rows, 1)

    def to_tokens(rows):
        return exchange(rows, -1)

    slot_gates = jnp.zeros((slot_count,), jnp.float32)
    for r, chosen in enumerate(route_maps):
        slot_gates = slot_gates + jnp.sum(jnp.where(chosen, route_gates[:, r][:, None], 0.0), axis=0)
    got_x = to_experts(with_cols(place(tokens), slot_gates, pad))
    gate_column = join_f32(got_x[:, col_width], got_x[:, col_width + 1])[:, None]
    rows_in = gather_blocks(got_x[:, :col_width], n_ctx, me)
    got_dy = to_experts(place(cotangent))
    grads_in = gather_blocks(got_dy, n_ctx, me)

    group = w_gate.shape[2]
    gate_w = w_gate[0].reshape(n_ctx, col_width, group)
    up_w = w_up[0].reshape(n_ctx, col_width, group)
    down_w = w_down[0]
    down_cols = [down_w[:, q * col_width : (q + 1) * col_width] for q in range(n_ctx)]

    pre_gate = jnp.einsum("nsd,ndf->sf", rows_in, gate_w, preferred_element_type=jnp.float32)
    pre_up = jnp.einsum("nsd,ndf->sf", rows_in, up_w, preferred_element_type=jnp.float32)
    sigma = jax.nn.sigmoid(pre_gate)
    activated = pre_gate * sigma
    hidden = (activated * pre_up).astype(jnp.bfloat16)
    partial_out = jnp.stack(
        [jnp.dot(hidden, cols, preferred_element_type=jnp.float32) for cols in down_cols]
    ).astype(jnp.bfloat16)
    gate_part = jnp.einsum(
        "nsd,nsd->s", partial_out.astype(jnp.float32), grads_in.astype(jnp.float32)
    )
    expert_out = scatter_sum(partial_out.astype(jnp.float32), n_ctx, me).astype(jnp.bfloat16)
    gate_sum = all_sum(gate_part, n_ctx)
    back_out = to_tokens(with_cols(expert_out, gate_sum, pad))

    contract_last = (((1,), (1,)), ((), ()))
    down_t = sum(
        lax.dot_general(grads_in[q], down_cols[q], contract_last, preferred_element_type=jnp.float32)
        for q in range(n_ctx)
    )
    hidden_grad = gate_column * down_t
    grad_gate = (hidden_grad * pre_up * sigma * (1.0 + pre_gate * (1.0 - sigma))).astype(
        jnp.bfloat16
    )
    grad_up = (hidden_grad * activated).astype(jnp.bfloat16)
    back_terms = jnp.einsum(
        "sf,ndf->nsd", grad_gate, gate_w, preferred_element_type=jnp.float32
    ) + jnp.einsum("sf,ndf->nsd", grad_up, up_w, preferred_element_type=jnp.float32)
    back_terms = back_terms.astype(jnp.bfloat16).astype(jnp.float32)
    slot_grad = scatter_sum(back_terms, n_ctx, me).astype(jnp.bfloat16)
    back_grad = to_tokens(slot_grad)

    w_gate_grad = jnp.einsum(
        "nsd,sf->ndf", rows_in, grad_gate, preferred_element_type=jnp.float32
    ).astype(jnp.bfloat16).reshape(1, n_ctx * col_width, group)
    w_up_grad = jnp.einsum(
        "nsd,sf->ndf", rows_in, grad_up, preferred_element_type=jnp.float32
    ).astype(jnp.bfloat16).reshape(1, n_ctx * col_width, group)

    slot_gg = join_f32(back_out[:, col_width], back_out[:, col_width + 1])
    out_rows = back_out[:, :col_width]
    layer_out = jnp.zeros((tok_rows, col_width), jnp.float32)
    input_grad = jnp.zeros((tok_rows, col_width), jnp.float32)
    gate_terms = []
    for r, chosen in enumerate(route_maps):
        pick = chosen.astype(jnp.bfloat16)
        rows_r = jnp.dot(pick, out_rows, preferred_element_type=jnp.float32)
        layer_out = layer_out + route_gates[:, r][:, None] * rows_r
        input_grad = input_grad + jnp.dot(pick, back_grad, preferred_element_type=jnp.float32)
        gate_terms.append(jnp.sum(jnp.where(chosen, slot_gg[None, :], 0.0), axis=1))
    gate_grad = jnp.stack(gate_terms, axis=1)
    return (
        layer_out.astype(jnp.bfloat16),
        input_grad.astype(jnp.bfloat16),
        gate_grad,
        w_gate_grad,
        w_up_grad,
    )


def solution(mesh):
    in_specs = (
        P("ep", "ctx"),
        P("ep", "ctx"),
        P("ep", None),
        P("ep", None),
        P("ep", None, "ctx"),
        P("ep", None, "ctx"),
        P("ep", "ctx", None),
    )
    out_specs = (
        P("ep", "ctx"),
        P("ep", "ctx"),
        P("ep", None),
        P("ep", None, "ctx"),
        P("ep", None, "ctx"),
    )
    return jax.shard_map(shards, mesh=mesh, in_specs=in_specs, out_specs=out_specs, check_vma=False)
```

```python
import jax
import jax.numpy as jnp
from jax import lax
from jax.sharding import PartitionSpec as P


def route_onehot(expert_ids, experts, capacity):
    tok_rows, routes = expert_ids.shape
    flat_ids = expert_ids.reshape(-1)
    labels = jnp.arange(experts, dtype=jnp.int32)
    onehot = (flat_ids[:, None] == labels[None, :]).astype(jnp.int32)
    earlier = jnp.cumsum(onehot, axis=0) - onehot
    slot_rank = jnp.sum(earlier * onehot, axis=1)
    slot_ids = (flat_ids * capacity + slot_rank).reshape(tok_rows, routes)
    positions = jnp.arange(experts * capacity, dtype=jnp.int32)
    return [slot_ids[:, r][:, None] == positions[None, :] for r in range(routes)]


def split_f32(values):
    hi = values.astype(jnp.bfloat16)
    lo = (values - hi.astype(jnp.float32)).astype(jnp.bfloat16)
    return hi, lo


def join_f32(hi, lo):
    return hi.astype(jnp.float32) + lo.astype(jnp.float32)


def ctx_bits(n_ctx):
    bits = n_ctx.bit_length() - 1
    assert 1 << bits == n_ctx
    return bits


def xor_pairs(n_ctx, bit):
    return [(i, i ^ (1 << bit)) for i in range(n_ctx)]


def gather_blocks(block, n_ctx, me):
    held = block[None]
    for bit in reversed(range(ctx_bits(n_ctx))):
        other = lax.ppermute(held, "ctx", xor_pairs(n_ctx, bit))
        mine_first = ((me >> bit) & 1) == 0
        pair = jnp.where(
            mine_first, jnp.stack([held, other], axis=1), jnp.stack([other, held], axis=1)
        )
        held = pair.reshape((-1,) + block.shape)
    return held


def scatter_sum(blocks, n_ctx, me, wait_for=None):
    acc = blocks
    for bit in range(ctx_bits(n_ctx)):
        halves = acc.reshape((-1, 2) + acc.shape[1:])
        keep_first = ((me >> bit) & 1) == 0
        keep = jnp.where(keep_first, halves[:, 0], halves[:, 1])
        send = jnp.where(keep_first, halves[:, 1], halves[:, 0]).astype(jnp.bfloat16)
        if bit == 1 and wait_for is not None:
            send, _ = lax.optimization_barrier((send, wait_for))
        got = lax.ppermute(send, "ctx", xor_pairs(n_ctx, bit))
        acc = keep + got.astype(jnp.float32)
    return acc[0]


def all_sum(values, n_ctx):
    for bit in range(ctx_bits(n_ctx)):
        values = values + lax.ppermute(values, "ctx", xor_pairs(n_ctx, bit))
    return values


def with_cols(rows, values, pad):
    hi, lo = split_f32(values)
    zeros = jnp.zeros((rows.shape[0], pad - 2), jnp.bfloat16)
    return jnp.concatenate([rows, hi[:, None], lo[:, None], zeros], axis=1)


def shards(tokens, cotangent, expert_ids, route_gates, w_gate, w_up, w_down):
    tok_rows, routes = expert_ids.shape
    experts = lax.axis_size("ep")
    n_ctx = lax.axis_size("ctx")
    me = lax.axis_index("ctx")
    capacity = 3 * tok_rows * routes // (2 * experts)
    slot_count = experts * capacity
    col_width = tokens.shape[1]
    pad = 128
    route_maps = route_onehot(expert_ids, experts, capacity)

    def place(values):
        placed = jnp.zeros((slot_count, values.shape[1]), jnp.float32)
        for chosen in route_maps:
            placed = placed + jnp.einsum(
                "ts,tc->sc", chosen.astype(jnp.bfloat16), values, preferred_element_type=jnp.float32
            )
        return placed.astype(jnp.bfloat16)

    def to_experts(rows):
        sent = rows.reshape(experts, capacity, rows.shape[1])
        got = lax.all_to_all(sent, "ep", split_axis=0, concat_axis=0, tiled=True)
        return got.reshape(slot_count, rows.shape[1])

    slot_gates = jnp.zeros((slot_count,), jnp.float32)
    for r, chosen in enumerate(route_maps):
        slot_gates = slot_gates + jnp.sum(jnp.where(chosen, route_gates[:, r][:, None], 0.0), axis=0)
    got_x = to_experts(with_cols(place(tokens), slot_gates, pad))
    gate_column = join_f32(got_x[:, col_width], got_x[:, col_width + 1])[:, None]
    rows_in = gather_blocks(got_x[:, :col_width], n_ctx, me)
    got_dy = to_experts(place(cotangent))
    grads_in = gather_blocks(got_dy, n_ctx, me)

    group = w_gate.shape[2]
    gate_w = w_gate[0].reshape(n_ctx, col_width, group)
    up_w = w_up[0].reshape(n_ctx, col_width, group)
    down_w = w_down[0]
    down_cols = [down_w[:, q * col_width : (q + 1) * col_width] for q in range(n_ctx)]

    pre_gate = jnp.einsum("nsd,ndf->sf", rows_in, gate_w, preferred_element_type=jnp.float32)
    pre_up = jnp.einsum("nsd,ndf->sf", rows_in, up_w, preferred_element_type=jnp.float32)
    sigma = jax.nn.sigmoid(pre_gate)
    activated = pre_gate * sigma
    hidden = (activated * pre_up).astype(jnp.bfloat16)
    partial_out = jnp.stack(
        [jnp.dot(hidden, cols, preferred_element_type=jnp.float32) for cols in down_cols]
    ).astype(jnp.bfloat16)
    gate_part = jnp.einsum(
        "nsd,nsd->s", partial_out.astype(jnp.float32), grads_in.astype(jnp.float32)
    )
    expert_out = scatter_sum(partial_out.astype(jnp.float32), n_ctx, me).astype(jnp.bfloat16)
    gate_sum = all_sum(gate_part, n_ctx)
    back_out = to_experts(with_cols(expert_out, gate_sum, pad))

    contract_last = (((1,), (1,)), ((), ()))
    down_t = sum(
        lax.dot_general(grads_in[q], down_cols[q], contract_last, preferred_element_type=jnp.float32)
        for q in range(n_ctx)
    )
    hidden_grad = gate_column * down_t
    grad_gate = (hidden_grad * pre_up * sigma * (1.0 + pre_gate * (1.0 - sigma))).astype(
        jnp.bfloat16
    )
    grad_up = (hidden_grad * activated).astype(jnp.bfloat16)
    back_terms = jnp.einsum(
        "sf,ndf->nsd", grad_gate, gate_w, preferred_element_type=jnp.float32
    ) + jnp.einsum("sf,ndf->nsd", grad_up, up_w, preferred_element_type=jnp.float32)
    back_terms = back_terms.astype(jnp.bfloat16).astype(jnp.float32)
    slot_grad = scatter_sum(back_terms, n_ctx, me, expert_out).astype(jnp.bfloat16)
    back_grad = to_experts(slot_grad)

    w_gate_grad = jnp.einsum(
        "nsd,sf->ndf", rows_in, grad_gate, preferred_element_type=jnp.float32
    ).astype(jnp.bfloat16).reshape(1, n_ctx * col_width, group)
    w_up_grad = jnp.einsum(
        "nsd,sf->ndf", rows_in, grad_up, preferred_element_type=jnp.float32
    ).astype(jnp.bfloat16).reshape(1, n_ctx * col_width, group)

    slot_gg = join_f32(back_out[:, col_width], back_out[:, col_width + 1])
    out_rows = back_out[:, :col_width]
    layer_out = jnp.zeros((tok_rows, col_width), jnp.float32)
    input_grad = jnp.zeros((tok_rows, col_width), jnp.float32)
    gate_terms = []
    for r, chosen in enumerate(route_maps):
        pick = chosen.astype(jnp.bfloat16)
        rows_r = jnp.dot(pick, out_rows, preferred_element_type=jnp.float32)
        layer_out = layer_out + route_gates[:, r][:, None] * rows_r
        input_grad = input_grad + jnp.dot(pick, back_grad, preferred_element_type=jnp.float32)
        gate_terms.append(jnp.sum(jnp.where(chosen, slot_gg[None, :], 0.0), axis=1))
    gate_grad = jnp.stack(gate_terms, axis=1)
    return (
        layer_out.astype(jnp.bfloat16),
        input_grad.astype(jnp.bfloat16),
        gate_grad,
        w_gate_grad,
        w_up_grad,
    )


def solution(mesh):
    in_specs = (
        P("ep", "ctx"),
        P("ep", "ctx"),
        P("ep", None),
        P("ep", None),
        P("ep", None, "ctx"),
        P("ep", None, "ctx"),
        P("ep", "ctx", None),
    )
    out_specs = (
        P("ep", "ctx"),
        P("ep", "ctx"),
        P("ep", None),
        P("ep", None, "ctx"),
        P("ep", None, "ctx"),
    )
    return jax.shard_map(shards, mesh=mesh, in_specs=in_specs, out_specs=out_specs, check_vma=False)
```

```python
import jax
import jax.numpy as jnp
from jax import lax
from jax.sharding import PartitionSpec as P


def route_onehot(expert_ids, experts, capacity):
    tok_rows, routes = expert_ids.shape
    flat_ids = expert_ids.reshape(-1)
    labels = jnp.arange(experts, dtype=jnp.int32)
    onehot = (flat_ids[:, None] == labels[None, :]).astype(jnp.int32)
    earlier = jnp.cumsum(onehot, axis=0) - onehot
    slot_rank = jnp.sum(earlier * onehot, axis=1)
    slot_ids = (flat_ids * capacity + slot_rank).reshape(tok_rows, routes)
    positions = jnp.arange(experts * capacity, dtype=jnp.int32)
    return [slot_ids[:, r][:, None] == positions[None, :] for r in range(routes)]


def split_f32(values):
    hi = values.astype(jnp.bfloat16)
    lo = (values - hi.astype(jnp.float32)).astype(jnp.bfloat16)
    return hi, lo


def join_f32(hi, lo):
    return hi.astype(jnp.float32) + lo.astype(jnp.float32)


def ctx_bits(n_ctx):
    bits = n_ctx.bit_length() - 1
    assert 1 << bits == n_ctx
    return bits


def xor_pairs(n_ctx, bit):
    return [(i, i ^ (1 << bit)) for i in range(n_ctx)]


def gather_blocks(block, n_ctx, me):
    held = block[None]
    for bit in reversed(range(ctx_bits(n_ctx))):
        other = lax.ppermute(held, "ctx", xor_pairs(n_ctx, bit))
        mine_first = ((me >> bit) & 1) == 0
        pair = jnp.where(
            mine_first, jnp.stack([held, other], axis=1), jnp.stack([other, held], axis=1)
        )
        held = pair.reshape((-1,) + block.shape)
    return held


def after(values, *needed):
    zero = sum(jnp.ravel(x)[0].astype(jnp.float32) for x in needed) * 0.0
    return values + zero.astype(values.dtype)


def scatter_sum(blocks, n_ctx, me, wait_for=None, stages=None):
    acc = blocks
    for bit in range(ctx_bits(n_ctx)):
        halves = acc.reshape((-1, 2) + acc.shape[1:])
        keep_first = ((me >> bit) & 1) == 0
        keep = jnp.where(keep_first, halves[:, 0], halves[:, 1])
        send = jnp.where(keep_first, halves[:, 1], halves[:, 0]).astype(jnp.bfloat16)
        if bit == 1 and wait_for is not None:
            send = after(send, wait_for)
        got = lax.ppermute(send, "ctx", xor_pairs(n_ctx, bit))
        acc = keep + got.astype(jnp.float32)
        if stages is not None:
            stages.append(acc)
    return acc[0]


def all_sum(values, n_ctx):
    for bit in range(ctx_bits(n_ctx)):
        values = values + lax.ppermute(values, "ctx", xor_pairs(n_ctx, bit))
    return values


def with_cols(rows, values, pad):
    hi, lo = split_f32(values)
    zeros = jnp.zeros((rows.shape[0], pad - 2), jnp.bfloat16)
    return jnp.concatenate([rows, hi[:, None], lo[:, None], zeros], axis=1)


def shards(tokens, cotangent, expert_ids, route_gates, w_gate, w_up, w_down):
    tok_rows, routes = expert_ids.shape
    experts = lax.axis_size("ep")
    n_ctx = lax.axis_size("ctx")
    me = lax.axis_index("ctx")
    capacity = 3 * tok_rows * routes // (2 * experts)
    slot_count = experts * capacity
    col_width = tokens.shape[1]
    pad = 128
    route_maps = route_onehot(expert_ids, experts, capacity)

    def place(values):
        placed = jnp.zeros((slot_count, values.shape[1]), jnp.float32)
        for chosen in route_maps:
            placed = placed + jnp.einsum(
                "ts,tc->sc", chosen.astype(jnp.bfloat16), values, preferred_element_type=jnp.float32
            )
        return placed.astype(jnp.bfloat16)

    def to_experts(rows):
        sent = rows.reshape(experts, capacity, rows.shape[1])
        got = lax.all_to_all(sent, "ep", split_axis=0, concat_axis=0, tiled=True)
        return got.reshape(slot_count, rows.shape[1])

    slot_gates = jnp.zeros((slot_count,), jnp.float32)
    for r, chosen in enumerate(route_maps):
        slot_gates = slot_gates + jnp.sum(jnp.where(chosen, route_gates[:, r][:, None], 0.0), axis=0)
    got_x = to_experts(with_cols(place(tokens), slot_gates, pad))
    gate_column = join_f32(got_x[:, col_width], got_x[:, col_width + 1])[:, None]
    rows_in = gather_blocks(got_x[:, :col_width], n_ctx, me)
    got_dy = to_experts(place(cotangent))
    grads_in = gather_blocks(after(got_dy, rows_in), n_ctx, me)

    group = w_gate.shape[2]
    gate_w = w_gate[0].reshape(n_ctx, col_width, group)
    up_w = w_up[0].reshape(n_ctx, col_width, group)
    down_w = w_down[0]
    down_cols = [down_w[:, q * col_width : (q + 1) * col_width] for q in range(n_ctx)]

    pre_gate = jnp.einsum("nsd,ndf->sf", rows_in, gate_w, preferred_element_type=jnp.float32)
    pre_up = jnp.einsum("nsd,ndf->sf", rows_in, up_w, preferred_element_type=jnp.float32)
    sigma = jax.nn.sigmoid(pre_gate)
    activated = pre_gate * sigma
    hidden = (activated * pre_up).astype(jnp.bfloat16)
    partial_out = jnp.stack(
        [jnp.dot(hidden, cols, preferred_element_type=jnp.float32) for cols in down_cols]
    ).astype(jnp.bfloat16)
    gate_part = jnp.einsum(
        "nsd,nsd->s", partial_out.astype(jnp.float32), grads_in.astype(jnp.float32)
    )
    out_stages = []
    expert_out = scatter_sum(
        partial_out.astype(jnp.float32), n_ctx, me, stages=out_stages
    ).astype(jnp.bfloat16)
    gate_sum = all_sum(gate_part, n_ctx)
    back_out = to_experts(with_cols(expert_out, gate_sum, pad))

    contract_last = (((1,), (1,)), ((), ()))
    down_t = sum(
        lax.dot_general(grads_in[q], down_cols[q], contract_last, preferred_element_type=jnp.float32)
        for q in range(n_ctx)
    )
    hidden_grad = after(gate_column * down_t, out_stages[0])
    grad_gate = (hidden_grad * pre_up * sigma * (1.0 + pre_gate * (1.0 - sigma))).astype(
        jnp.bfloat16
    )
    grad_up = (hidden_grad * activated).astype(jnp.bfloat16)
    back_terms = jnp.einsum(
        "sf,ndf->nsd", grad_gate, gate_w, preferred_element_type=jnp.float32
    ) + jnp.einsum("sf,ndf->nsd", grad_up, up_w, preferred_element_type=jnp.float32)
    back_terms = back_terms.astype(jnp.bfloat16).astype(jnp.float32)
    slot_grad = scatter_sum(back_terms, n_ctx, me, expert_out).astype(jnp.bfloat16)
    back_grad = to_experts(slot_grad)

    w_gate_grad = jnp.einsum(
        "nsd,sf->ndf", rows_in, grad_gate, preferred_element_type=jnp.float32
    ).astype(jnp.bfloat16).reshape(1, n_ctx * col_width, group)
    w_up_grad = jnp.einsum(
        "nsd,sf->ndf", rows_in, grad_up, preferred_element_type=jnp.float32
    ).astype(jnp.bfloat16).reshape(1, n_ctx * col_width, group)

    slot_gg = join_f32(back_out[:, col_width], back_out[:, col_width + 1])
    out_rows = back_out[:, :col_width]
    layer_out = jnp.zeros((tok_rows, col_width), jnp.float32)
    input_grad = jnp.zeros((tok_rows, col_width), jnp.float32)
    gate_terms = []
    for r, chosen in enumerate(route_maps):
        pick = chosen.astype(jnp.bfloat16)
        rows_r = jnp.dot(pick, out_rows, preferred_element_type=jnp.float32)
        layer_out = layer_out + route_gates[:, r][:, None] * rows_r
        input_grad = input_grad + jnp.dot(pick, back_grad, preferred_element_type=jnp.float32)
        gate_terms.append(jnp.sum(jnp.where(chosen, slot_gg[None, :], 0.0), axis=1))
    gate_grad = jnp.stack(gate_terms, axis=1)
    return (
        layer_out.astype(jnp.bfloat16),
        input_grad.astype(jnp.bfloat16),
        gate_grad,
        w_gate_grad,
        w_up_grad,
    )


def solution(mesh):
    in_specs = (
        P("ep", "ctx"),
        P("ep", "ctx"),
        P("ep", None),
        P("ep", None),
        P("ep", None, "ctx"),
        P("ep", None, "ctx"),
        P("ep", "ctx", None),
    )
    out_specs = (
        P("ep", "ctx"),
        P("ep", "ctx"),
        P("ep", None),
        P("ep", None, "ctx"),
        P("ep", None, "ctx"),
    )
    return jax.shard_map(shards, mesh=mesh, in_specs=in_specs, out_specs=out_specs, check_vma=False)
```

```python
import jax
import jax.numpy as jnp
from jax import lax
from jax.sharding import PartitionSpec as P


def route_onehot(expert_ids, experts, capacity):
    tok_rows, routes = expert_ids.shape
    flat_ids = expert_ids.reshape(-1)
    labels = jnp.arange(experts, dtype=jnp.int32)
    onehot = (flat_ids[:, None] == labels[None, :]).astype(jnp.int32)
    earlier = jnp.cumsum(onehot, axis=0) - onehot
    slot_rank = jnp.sum(earlier * onehot, axis=1)
    slot_ids = (flat_ids * capacity + slot_rank).reshape(tok_rows, routes)
    positions = jnp.arange(experts * capacity, dtype=jnp.int32)
    return [slot_ids[:, r][:, None] == positions[None, :] for r in range(routes)]


def split_f32(values):
    hi = values.astype(jnp.bfloat16)
    lo = (values - hi.astype(jnp.float32)).astype(jnp.bfloat16)
    return hi, lo


def join_f32(hi, lo):
    return hi.astype(jnp.float32) + lo.astype(jnp.float32)


def ctx_bits(n_ctx):
    bits = n_ctx.bit_length() - 1
    assert 1 << bits == n_ctx
    return bits


def xor_pairs(n_ctx, bit):
    return [(i, i ^ (1 << bit)) for i in range(n_ctx)]


def gather_blocks(block, n_ctx, me):
    held = block[None]
    for bit in reversed(range(ctx_bits(n_ctx))):
        other = lax.ppermute(held, "ctx", xor_pairs(n_ctx, bit))
        mine_first = ((me >> bit) & 1) == 0
        pair = jnp.where(
            mine_first, jnp.stack([held, other], axis=1), jnp.stack([other, held], axis=1)
        )
        held = pair.reshape((-1,) + block.shape)
    return held


def after(values, *needed):
    zero = sum(jnp.ravel(x)[0].astype(jnp.float32) for x in needed) * 0.0
    return values + zero.astype(values.dtype)


def scatter_sum(blocks, n_ctx, me, wait_for=None):
    acc = blocks
    for bit in range(ctx_bits(n_ctx)):
        halves = acc.reshape((-1, 2) + acc.shape[1:])
        keep_first = ((me >> bit) & 1) == 0
        keep = jnp.where(keep_first, halves[:, 0], halves[:, 1])
        send = jnp.where(keep_first, halves[:, 1], halves[:, 0]).astype(jnp.bfloat16)
        if bit == 1 and wait_for is not None:
            send = after(send, wait_for)
        got = lax.ppermute(send, "ctx", xor_pairs(n_ctx, bit))
        acc = keep + got.astype(jnp.float32)
    return acc[0]


def all_sum(values, n_ctx):
    for bit in range(ctx_bits(n_ctx)):
        values = values + lax.ppermute(values, "ctx", xor_pairs(n_ctx, bit))
    return values


def with_cols(rows, values, pad):
    hi, lo = split_f32(values)
    zeros = jnp.zeros((rows.shape[0], pad - 2), jnp.bfloat16)
    return jnp.concatenate([rows, hi[:, None], lo[:, None], zeros], axis=1)


def shards(tokens, cotangent, expert_ids, route_gates, w_gate, w_up, w_down):
    tok_rows, routes = expert_ids.shape
    experts = lax.axis_size("ep")
    n_ctx = lax.axis_size("ctx")
    me = lax.axis_index("ctx")
    capacity = 3 * tok_rows * routes // (2 * experts)
    slot_count = experts * capacity
    col_width = tokens.shape[1]
    pad = 128
    route_maps = route_onehot(expert_ids, experts, capacity)

    def place(values):
        placed = jnp.zeros((slot_count, values.shape[1]), jnp.float32)
        for chosen in route_maps:
            placed = placed + jnp.einsum(
                "ts,tc->sc", chosen.astype(jnp.bfloat16), values, preferred_element_type=jnp.float32
            )
        return placed.astype(jnp.bfloat16)

    def to_experts(rows):
        sent = rows.reshape(experts, capacity, rows.shape[1])
        got = lax.all_to_all(sent, "ep", split_axis=0, concat_axis=0, tiled=True)
        return got.reshape(slot_count, rows.shape[1])

    slot_gates = jnp.zeros((slot_count,), jnp.float32)
    for r, chosen in enumerate(route_maps):
        slot_gates = slot_gates + jnp.sum(jnp.where(chosen, route_gates[:, r][:, None], 0.0), axis=0)
    got_x = to_experts(with_cols(place(tokens), slot_gates, pad))
    gate_column = join_f32(got_x[:, col_width], got_x[:, col_width + 1])[:, None]
    rows_in = gather_blocks(got_x[:, :col_width], n_ctx, me)
    got_dy = to_experts(place(cotangent))
    grads_in = gather_blocks(got_dy, n_ctx, me)

    group = w_gate.shape[2]
    gate_w = w_gate[0].reshape(n_ctx, col_width, group)
    up_w = w_up[0].reshape(n_ctx, col_width, group)
    down_w = w_down[0]
    down_cols = [down_w[:, q * col_width : (q + 1) * col_width] for q in range(n_ctx)]

    pre_gate = jnp.einsum("nsd,ndf->sf", rows_in, gate_w, preferred_element_type=jnp.float32)
    pre_up = jnp.einsum("nsd,ndf->sf", rows_in, up_w, preferred_element_type=jnp.float32)
    sigma = jax.nn.sigmoid(pre_gate)
    activated = pre_gate * sigma
    hidden = (activated * pre_up).astype(jnp.bfloat16)
    partial_out = jnp.stack(
        [jnp.dot(hidden, cols, preferred_element_type=jnp.float32) for cols in down_cols]
    ).astype(jnp.bfloat16)
    gate_part = jnp.einsum(
        "nsd,nsd->s", partial_out.astype(jnp.float32), grads_in.astype(jnp.float32)
    )
    expert_out = scatter_sum(partial_out.astype(jnp.float32), n_ctx, me).astype(jnp.bfloat16)
    gate_sum = all_sum(gate_part, n_ctx)
    back_out = to_experts(with_cols(expert_out, gate_sum, pad))

    contract_last = (((1,), (1,)), ((), ()))
    down_t = sum(
        lax.dot_general(grads_in[q], down_cols[q], contract_last, preferred_element_type=jnp.float32)
        for q in range(n_ctx)
    )
    hidden_grad = gate_column * down_t
    grad_gate = (hidden_grad * pre_up * sigma * (1.0 + pre_gate * (1.0 - sigma))).astype(
        jnp.bfloat16
    )
    grad_up = (hidden_grad * activated).astype(jnp.bfloat16)
    back_terms = jnp.einsum(
        "sf,ndf->nsd", grad_gate, gate_w, preferred_element_type=jnp.float32
    ) + jnp.einsum("sf,ndf->nsd", grad_up, up_w, preferred_element_type=jnp.float32)
    back_terms = back_terms.astype(jnp.bfloat16).astype(jnp.float32)
    slot_grad = scatter_sum(back_terms, n_ctx, me, expert_out).astype(jnp.bfloat16)
    back_grad = to_experts(slot_grad)

    w_gate_grad = jnp.einsum(
        "nsd,sf->ndf", rows_in, grad_gate, preferred_element_type=jnp.float32
    ).astype(jnp.bfloat16).reshape(1, n_ctx * col_width, group)
    w_up_grad = jnp.einsum(
        "nsd,sf->ndf", rows_in, grad_up, preferred_element_type=jnp.float32
    ).astype(jnp.bfloat16).reshape(1, n_ctx * col_width, group)

    slot_gg = join_f32(back_out[:, col_width], back_out[:, col_width + 1])
    out_rows = back_out[:, :col_width]
    layer_out = jnp.zeros((tok_rows, col_width), jnp.float32)
    input_grad = jnp.zeros((tok_rows, col_width), jnp.float32)
    gate_terms = []
    for r, chosen in enumerate(route_maps):
        pick = chosen.astype(jnp.bfloat16)
        rows_r = jnp.dot(pick, out_rows, preferred_element_type=jnp.float32)
        layer_out = layer_out + route_gates[:, r][:, None] * rows_r
        input_grad = input_grad + jnp.dot(pick, back_grad, preferred_element_type=jnp.float32)
        gate_terms.append(jnp.sum(jnp.where(chosen, slot_gg[None, :], 0.0), axis=1))
    gate_grad = jnp.stack(gate_terms, axis=1)
    return (
        layer_out.astype(jnp.bfloat16),
        input_grad.astype(jnp.bfloat16),
        gate_grad,
        w_gate_grad,
        w_up_grad,
    )


def solution(mesh):
    in_specs = (
        P("ep", "ctx"),
        P("ep", "ctx"),
        P("ep", None),
        P("ep", None),
        P("ep", None, "ctx"),
        P("ep", None, "ctx"),
        P("ep", "ctx", None),
    )
    out_specs = (
        P("ep", "ctx"),
        P("ep", "ctx"),
        P("ep", None),
        P("ep", None, "ctx"),
        P("ep", None, "ctx"),
    )
    return jax.shard_map(shards, mesh=mesh, in_specs=in_specs, out_specs=out_specs, check_vma=False)
```

```python
import jax
import jax.numpy as jnp
from jax import lax
from jax.sharding import PartitionSpec as P


def route_onehot(expert_ids, experts, capacity):
    tok_rows, routes = expert_ids.shape
    flat_ids = expert_ids.reshape(-1)
    labels = jnp.arange(experts, dtype=jnp.int32)
    onehot = (flat_ids[:, None] == labels[None, :]).astype(jnp.int32)
    earlier = jnp.cumsum(onehot, axis=0) - onehot
    slot_rank = jnp.sum(earlier * onehot, axis=1)
    slot_ids = (flat_ids * capacity + slot_rank).reshape(tok_rows, routes)
    positions = jnp.arange(experts * capacity, dtype=jnp.int32)
    return [slot_ids[:, r][:, None] == positions[None, :] for r in range(routes)]


def split_f32(values):
    hi = values.astype(jnp.bfloat16)
    lo = (values - hi.astype(jnp.float32)).astype(jnp.bfloat16)
    return hi, lo


def join_f32(hi, lo):
    return hi.astype(jnp.float32) + lo.astype(jnp.float32)


def ctx_bits(n_ctx):
    bits = n_ctx.bit_length() - 1
    assert 1 << bits == n_ctx
    return bits


def xor_pairs(n_ctx, bit):
    return [(i, i ^ (1 << bit)) for i in range(n_ctx)]


def gather_blocks(block, n_ctx, me):
    held = block[None]
    for bit in reversed(range(ctx_bits(n_ctx))):
        other = lax.ppermute(held, "ctx", xor_pairs(n_ctx, bit))
        mine_first = ((me >> bit) & 1) == 0
        pair = jnp.where(
            mine_first, jnp.stack([held, other], axis=1), jnp.stack([other, held], axis=1)
        )
        held = pair.reshape((-1,) + block.shape)
    return held


def after(values, *needed):
    zero = sum(jnp.ravel(x)[0].astype(jnp.float32) for x in needed) * 0.0
    return values + zero.astype(values.dtype)


def scatter_sum(blocks, n_ctx, me, wait_for=None):
    acc = blocks
    for bit in range(ctx_bits(n_ctx)):
        halves = acc.reshape((-1, 2) + acc.shape[1:])
        keep_first = ((me >> bit) & 1) == 0
        keep = jnp.where(keep_first, halves[:, 0], halves[:, 1])
        send = jnp.where(keep_first, halves[:, 1], halves[:, 0]).astype(jnp.bfloat16)
        if bit == 1 and wait_for is not None:
            send = after(send, wait_for)
        got = lax.ppermute(send, "ctx", xor_pairs(n_ctx, bit))
        acc = keep + got.astype(jnp.float32)
    return acc[0]


def all_sum(values, n_ctx):
    for bit in range(ctx_bits(n_ctx)):
        values = values + lax.ppermute(values, "ctx", xor_pairs(n_ctx, bit))
    return values


def with_cols(rows, values, pad):
    hi, lo = split_f32(values)
    zeros = jnp.zeros((rows.shape[0], pad - 2), jnp.bfloat16)
    return jnp.concatenate([rows, hi[:, None], lo[:, None], zeros], axis=1)


def shards(tokens, cotangent, expert_ids, route_gates, w_gate, w_up, w_down):
    tok_rows, routes = expert_ids.shape
    experts = lax.axis_size("ep")
    n_ctx = lax.axis_size("ctx")
    me = lax.axis_index("ctx")
    capacity = 3 * tok_rows * routes // (2 * experts)
    slot_count = experts * capacity
    col_width = tokens.shape[1]
    pad = 128
    route_maps = route_onehot(expert_ids, experts, capacity)

    def place(values):
        placed = jnp.zeros((slot_count, values.shape[1]), jnp.float32)
        for chosen in route_maps:
            placed = placed + jnp.einsum(
                "ts,tc->sc", chosen.astype(jnp.bfloat16), values, preferred_element_type=jnp.float32
            )
        return placed.astype(jnp.bfloat16)

    def to_experts(rows):
        sent = rows.reshape(experts, capacity, rows.shape[1])
        got = lax.all_to_all(sent, "ep", split_axis=0, concat_axis=0, tiled=True)
        return got.reshape(slot_count, rows.shape[1])

    slot_gates = jnp.zeros((slot_count,), jnp.float32)
    for r, chosen in enumerate(route_maps):
        slot_gates = slot_gates + jnp.sum(jnp.where(chosen, route_gates[:, r][:, None], 0.0), axis=0)
    got_x = to_experts(with_cols(place(tokens), slot_gates, pad))
    gate_column = join_f32(got_x[:, col_width], got_x[:, col_width + 1])[:, None]
    rows_in = gather_blocks(got_x[:, :col_width], n_ctx, me)
    got_dy = to_experts(place(cotangent))
    grads_in = gather_blocks(got_dy, n_ctx, me)

    group = w_gate.shape[2]
    gate_w = w_gate[0].reshape(n_ctx, col_width, group)
    up_w = w_up[0].reshape(n_ctx, col_width, group)
    down_w = w_down[0]
    down_cols = [down_w[:, q * col_width : (q + 1) * col_width] for q in range(n_ctx)]

    pre_gate = jnp.einsum("nsd,ndf->sf", rows_in, gate_w, preferred_element_type=jnp.float32)
    pre_up = jnp.einsum("nsd,ndf->sf", rows_in, up_w, preferred_element_type=jnp.float32)
    sigma = jax.nn.sigmoid(pre_gate)
    activated = pre_gate * sigma
    hidden = (activated * pre_up).astype(jnp.bfloat16)
    partial_out = jnp.stack(
        [jnp.dot(hidden, cols, preferred_element_type=jnp.float32) for cols in down_cols]
    ).astype(jnp.bfloat16)
    gate_part = jnp.einsum(
        "nsd,nsd->s", partial_out.astype(jnp.float32), grads_in.astype(jnp.float32)
    )
    gate_sum = all_sum(gate_part, n_ctx)

    contract_last = (((1,), (1,)), ((), ()))
    down_t = sum(
        lax.dot_general(grads_in[q], down_cols[q], contract_last, preferred_element_type=jnp.float32)
        for q in range(n_ctx)
    )
    hidden_grad = gate_column * down_t
    grad_gate = (hidden_grad * pre_up * sigma * (1.0 + pre_gate * (1.0 - sigma))).astype(
        jnp.bfloat16
    )
    grad_up = (hidden_grad * activated).astype(jnp.bfloat16)
    back_terms = jnp.einsum(
        "sf,ndf->nsd", grad_gate, gate_w, preferred_element_type=jnp.float32
    ) + jnp.einsum("sf,ndf->nsd", grad_up, up_w, preferred_element_type=jnp.float32)
    back_terms = back_terms.astype(jnp.bfloat16).astype(jnp.float32)
    slot_grad = scatter_sum(back_terms, n_ctx, me).astype(jnp.bfloat16)
    back_grad = to_experts(slot_grad)
    expert_out = scatter_sum(
        partial_out.astype(jnp.float32), n_ctx, me, slot_grad
    ).astype(jnp.bfloat16)
    back_out = to_experts(with_cols(expert_out, gate_sum, pad))

    w_gate_grad = jnp.einsum(
        "nsd,sf->ndf", rows_in, grad_gate, preferred_element_type=jnp.float32
    ).astype(jnp.bfloat16).reshape(1, n_ctx * col_width, group)
    w_up_grad = jnp.einsum(
        "nsd,sf->ndf", rows_in, grad_up, preferred_element_type=jnp.float32
    ).astype(jnp.bfloat16).reshape(1, n_ctx * col_width, group)

    slot_gg = join_f32(back_out[:, col_width], back_out[:, col_width + 1])
    out_rows = back_out[:, :col_width]
    layer_out = jnp.zeros((tok_rows, col_width), jnp.float32)
    input_grad = jnp.zeros((tok_rows, col_width), jnp.float32)
    gate_terms = []
    for r, chosen in enumerate(route_maps):
        pick = chosen.astype(jnp.bfloat16)
        rows_r = jnp.dot(pick, out_rows, preferred_element_type=jnp.float32)
        layer_out = layer_out + route_gates[:, r][:, None] * rows_r
        input_grad = input_grad + jnp.dot(pick, back_grad, preferred_element_type=jnp.float32)
        gate_terms.append(jnp.sum(jnp.where(chosen, slot_gg[None, :], 0.0), axis=1))
    gate_grad = jnp.stack(gate_terms, axis=1)
    return (
        layer_out.astype(jnp.bfloat16),
        input_grad.astype(jnp.bfloat16),
        gate_grad,
        w_gate_grad,
        w_up_grad,
    )


def solution(mesh):
    in_specs = (
        P("ep", "ctx"),
        P("ep", "ctx"),
        P("ep", None),
        P("ep", None),
        P("ep", None, "ctx"),
        P("ep", None, "ctx"),
        P("ep", "ctx", None),
    )
    out_specs = (
        P("ep", "ctx"),
        P("ep", "ctx"),
        P("ep", None),
        P("ep", None, "ctx"),
        P("ep", None, "ctx"),
    )
    return jax.shard_map(shards, mesh=mesh, in_specs=in_specs, out_specs=out_specs, check_vma=False)
```

```python
import jax
import jax.numpy as jnp
from jax import lax
from jax.sharding import PartitionSpec as P


def route_onehot(expert_ids, experts, capacity):
    tok_rows, routes = expert_ids.shape
    flat_ids = expert_ids.reshape(-1)
    labels = jnp.arange(experts, dtype=jnp.int32)
    onehot = (flat_ids[:, None] == labels[None, :]).astype(jnp.bfloat16)
    pairs = jnp.arange(flat_ids.shape[0], dtype=jnp.int32)
    before = (pairs[:, None] > pairs[None, :]).astype(jnp.bfloat16)
    earlier = jnp.dot(before, onehot, preferred_element_type=jnp.float32)
    slot_rank = jnp.sum(earlier * onehot.astype(jnp.float32), axis=1).astype(jnp.int32)
    slot_ids = (flat_ids * capacity + slot_rank).reshape(tok_rows, routes)
    positions = jnp.arange(experts * capacity, dtype=jnp.int32)
    return [slot_ids[:, r][:, None] == positions[None, :] for r in range(routes)]


def split_f32(values):
    hi = values.astype(jnp.bfloat16)
    lo = (values - hi.astype(jnp.float32)).astype(jnp.bfloat16)
    return hi, lo


def join_f32(hi, lo):
    return hi.astype(jnp.float32) + lo.astype(jnp.float32)


def ctx_bits(n_ctx):
    bits = n_ctx.bit_length() - 1
    assert 1 << bits == n_ctx
    return bits


def xor_pairs(n_ctx, bit):
    return [(i, i ^ (1 << bit)) for i in range(n_ctx)]


def gather_blocks(block, n_ctx, me):
    held = block[None]
    for bit in reversed(range(ctx_bits(n_ctx))):
        other = lax.ppermute(held, "ctx", xor_pairs(n_ctx, bit))
        mine_first = ((me >> bit) & 1) == 0
        pair = jnp.where(
            mine_first, jnp.stack([held, other], axis=1), jnp.stack([other, held], axis=1)
        )
        held = pair.reshape((-1,) + block.shape)
    return held


def scatter_sum(blocks, n_ctx, me):
    acc = blocks
    for bit in range(ctx_bits(n_ctx)):
        halves = acc.reshape((-1, 2) + acc.shape[1:])
        keep_first = ((me >> bit) & 1) == 0
        keep = jnp.where(keep_first, halves[:, 0], halves[:, 1])
        send = jnp.where(keep_first, halves[:, 1], halves[:, 0]).astype(jnp.bfloat16)
        got = lax.ppermute(send, "ctx", xor_pairs(n_ctx, bit))
        acc = keep + got.astype(jnp.float32)
    return acc[0]


def all_sum(values, n_ctx):
    for bit in range(ctx_bits(n_ctx)):
        values = values + lax.ppermute(values, "ctx", xor_pairs(n_ctx, bit))
    return values


def with_cols(rows, values, pad):
    hi, lo = split_f32(values)
    zeros = jnp.zeros((rows.shape[0], pad - 2), jnp.bfloat16)
    return jnp.concatenate([rows, hi[:, None], lo[:, None], zeros], axis=1)


def shards(tokens, cotangent, expert_ids, route_gates, w_gate, w_up, w_down):
    tok_rows, routes = expert_ids.shape
    experts = lax.axis_size("ep")
    n_ctx = lax.axis_size("ctx")
    me = lax.axis_index("ctx")
    capacity = 3 * tok_rows * routes // (2 * experts)
    slot_count = experts * capacity
    col_width = tokens.shape[1]
    pad = 128
    route_maps = route_onehot(expert_ids, experts, capacity)

    def place(values):
        placed = jnp.zeros((slot_count, values.shape[1]), jnp.float32)
        for chosen in route_maps:
            placed = placed + jnp.einsum(
                "ts,tc->sc", chosen.astype(jnp.bfloat16), values, preferred_element_type=jnp.float32
            )
        return placed.astype(jnp.bfloat16)

    def to_experts(rows):
        sent = rows.reshape(experts, capacity, rows.shape[1])
        got = lax.all_to_all(sent, "ep", split_axis=0, concat_axis=0, tiled=True)
        return got.reshape(slot_count, rows.shape[1])

    slot_gates = jnp.zeros((slot_count,), jnp.float32)
    for r, chosen in enumerate(route_maps):
        slot_gates = slot_gates + jnp.sum(jnp.where(chosen, route_gates[:, r][:, None], 0.0), axis=0)
    got_x = to_experts(with_cols(place(tokens), slot_gates, pad))
    gate_column = join_f32(got_x[:, col_width], got_x[:, col_width + 1])[:, None]
    rows_in = gather_blocks(got_x[:, :col_width], n_ctx, me)
    got_dy = to_experts(place(cotangent))
    grads_in = gather_blocks(got_dy, n_ctx, me)

    group = w_gate.shape[2]
    gate_w = w_gate[0].reshape(n_ctx, col_width, group)
    up_w = w_up[0].reshape(n_ctx, col_width, group)
    down_w = w_down[0]
    down_cols = [down_w[:, q * col_width : (q + 1) * col_width] for q in range(n_ctx)]

    pre_gate = jnp.einsum("nsd,ndf->sf", rows_in, gate_w, preferred_element_type=jnp.float32)
    pre_up = jnp.einsum("nsd,ndf->sf", rows_in, up_w, preferred_element_type=jnp.float32)
    sigma = jax.nn.sigmoid(pre_gate)
    activated = pre_gate * sigma
    hidden = (activated * pre_up).astype(jnp.bfloat16)
    partial_out = jnp.stack(
        [jnp.dot(hidden, cols, preferred_element_type=jnp.float32) for cols in down_cols]
    ).astype(jnp.bfloat16)
    gate_part = jnp.einsum(
        "nsd,nsd->s", partial_out.astype(jnp.float32), grads_in.astype(jnp.float32)
    )
    expert_out = scatter_sum(partial_out.astype(jnp.float32), n_ctx, me).astype(jnp.bfloat16)
    gate_sum = all_sum(gate_part, n_ctx)
    back_out = to_experts(with_cols(expert_out, gate_sum, pad))

    contract_last = (((1,), (1,)), ((), ()))
    down_t = sum(
        lax.dot_general(grads_in[q], down_cols[q], contract_last, preferred_element_type=jnp.float32)
        for q in range(n_ctx)
    )
    hidden_grad = gate_column * down_t
    grad_gate = (hidden_grad * pre_up * sigma * (1.0 + pre_gate * (1.0 - sigma))).astype(
        jnp.bfloat16
    )
    grad_up = (hidden_grad * activated).astype(jnp.bfloat16)
    back_terms = jnp.einsum(
        "sf,ndf->nsd", grad_gate, gate_w, preferred_element_type=jnp.float32
    ) + jnp.einsum("sf,ndf->nsd", grad_up, up_w, preferred_element_type=jnp.float32)
    back_terms = back_terms.astype(jnp.bfloat16).astype(jnp.float32)
    slot_grad = scatter_sum(back_terms, n_ctx, me).astype(jnp.bfloat16)
    back_grad = to_experts(slot_grad)

    w_gate_grad = jnp.einsum(
        "nsd,sf->ndf", rows_in, grad_gate, preferred_element_type=jnp.float32
    ).astype(jnp.bfloat16).reshape(1, n_ctx * col_width, group)
    w_up_grad = jnp.einsum(
        "nsd,sf->ndf", rows_in, grad_up, preferred_element_type=jnp.float32
    ).astype(jnp.bfloat16).reshape(1, n_ctx * col_width, group)

    slot_gg = join_f32(back_out[:, col_width], back_out[:, col_width + 1])
    out_rows = back_out[:, :col_width]
    layer_out = jnp.zeros((tok_rows, col_width), jnp.float32)
    input_grad = jnp.zeros((tok_rows, col_width), jnp.float32)
    gate_terms = []
    for r, chosen in enumerate(route_maps):
        pick = chosen.astype(jnp.bfloat16)
        rows_r = jnp.dot(pick, out_rows, preferred_element_type=jnp.float32)
        layer_out = layer_out + route_gates[:, r][:, None] * rows_r
        input_grad = input_grad + jnp.dot(pick, back_grad, preferred_element_type=jnp.float32)
        gate_terms.append(jnp.sum(jnp.where(chosen, slot_gg[None, :], 0.0), axis=1))
    gate_grad = jnp.stack(gate_terms, axis=1)
    return (
        layer_out.astype(jnp.bfloat16),
        input_grad.astype(jnp.bfloat16),
        gate_grad,
        w_gate_grad,
        w_up_grad,
    )


def solution(mesh):
    in_specs = (
        P("ep", "ctx"),
        P("ep", "ctx"),
        P("ep", None),
        P("ep", None),
        P("ep", None, "ctx"),
        P("ep", None, "ctx"),
        P("ep", "ctx", None),
    )
    out_specs = (
        P("ep", "ctx"),
        P("ep", "ctx"),
        P("ep", None),
        P("ep", None, "ctx"),
        P("ep", None, "ctx"),
    )
    return jax.shard_map(shards, mesh=mesh, in_specs=in_specs, out_specs=out_specs, check_vma=False)
```

```python
import jax
import jax.numpy as jnp
from jax import lax
from jax.sharding import PartitionSpec as P


def route_onehot(expert_ids, experts, capacity):
    tok_rows, routes = expert_ids.shape
    flat_ids = expert_ids.reshape(-1)
    labels = jnp.arange(experts, dtype=jnp.int32)
    onehot = (flat_ids[:, None] == labels[None, :]).astype(jnp.bfloat16)
    pairs = jnp.arange(flat_ids.shape[0], dtype=jnp.int32)
    before = (pairs[:, None] > pairs[None, :]).astype(jnp.bfloat16)
    earlier = jnp.dot(before, onehot, preferred_element_type=jnp.float32)
    slot_rank = jnp.sum(earlier * onehot.astype(jnp.float32), axis=1).astype(jnp.int32)
    slot_ids = (flat_ids * capacity + slot_rank).reshape(tok_rows, routes)
    positions = jnp.arange(experts * capacity, dtype=jnp.int32)
    return [slot_ids[:, r][:, None] == positions[None, :] for r in range(routes)]


def split_f32(values):
    hi = values.astype(jnp.bfloat16)
    lo = (values - hi.astype(jnp.float32)).astype(jnp.bfloat16)
    return hi, lo


def join_f32(hi, lo):
    return hi.astype(jnp.float32) + lo.astype(jnp.float32)


def ctx_bits(n_ctx):
    bits = n_ctx.bit_length() - 1
    assert 1 << bits == n_ctx
    return bits


def xor_pairs(n_ctx, bit):
    return [(i, i ^ (1 << bit)) for i in range(n_ctx)]


def gather_blocks(block, n_ctx, me):
    held = block[None]
    for bit in reversed(range(ctx_bits(n_ctx))):
        other = lax.ppermute(held, "ctx", xor_pairs(n_ctx, bit))
        mine_first = ((me >> bit) & 1) == 0
        pair = jnp.where(
            mine_first, jnp.stack([held, other], axis=1), jnp.stack([other, held], axis=1)
        )
        held = pair.reshape((-1,) + block.shape)
    return held


def scatter_sum(blocks, n_ctx, me):
    acc = blocks
    for bit in range(ctx_bits(n_ctx)):
        halves = acc.reshape((-1, 2) + acc.shape[1:])
        keep_first = ((me >> bit) & 1) == 0
        keep = jnp.where(keep_first, halves[:, 0], halves[:, 1])
        send = jnp.where(keep_first, halves[:, 1], halves[:, 0]).astype(jnp.bfloat16)
        got = lax.ppermute(send, "ctx", xor_pairs(n_ctx, bit))
        acc = keep + got.astype(jnp.float32)
    return acc[0]


def all_sum(values, n_ctx):
    for bit in range(ctx_bits(n_ctx)):
        values = values + lax.ppermute(values, "ctx", xor_pairs(n_ctx, bit))
    return values


def with_cols(rows, values, pad):
    hi, lo = split_f32(values)
    zeros = jnp.zeros((rows.shape[0], pad - 2), jnp.bfloat16)
    return jnp.concatenate([rows, hi[:, None], lo[:, None], zeros], axis=1)


def shards(tokens, cotangent, expert_ids, route_gates, w_gate, w_up, w_down):
    tok_rows, routes = expert_ids.shape
    experts = lax.axis_size("ep")
    n_ctx = lax.axis_size("ctx")
    me = lax.axis_index("ctx")
    capacity = 3 * tok_rows * routes // (2 * experts)
    slot_count = experts * capacity
    col_width = tokens.shape[1]
    pad = 128
    route_maps = route_onehot(expert_ids, experts, capacity)

    def place(values):
        placed = jnp.zeros((slot_count, values.shape[1]), jnp.float32)
        for chosen in route_maps:
            placed = placed + jnp.einsum(
                "ts,tc->sc", chosen.astype(jnp.bfloat16), values, preferred_element_type=jnp.float32
            )
        return placed.astype(jnp.bfloat16)

    def to_experts(rows):
        sent = rows.reshape(experts, capacity, rows.shape[1])
        got = lax.all_to_all(sent, "ep", split_axis=0, concat_axis=0, tiled=True)
        return got.reshape(slot_count, rows.shape[1])

    slot_gates = jnp.zeros((slot_count,), jnp.float32)
    for r, chosen in enumerate(route_maps):
        slot_gates = slot_gates + jnp.sum(jnp.where(chosen, route_gates[:, r][:, None], 0.0), axis=0)
    got_x = to_experts(with_cols(place(tokens), slot_gates, pad))
    gate_column = join_f32(got_x[:, col_width], got_x[:, col_width + 1])[:, None]
    rows_in = gather_blocks(got_x[:, :col_width], n_ctx, me)
    got_dy = to_experts(place(cotangent))
    grads_in = gather_blocks(got_dy, n_ctx, me)

    group = w_gate.shape[2]
    gate_w = w_gate[0].reshape(n_ctx, col_width, group)
    up_w = w_up[0].reshape(n_ctx, col_width, group)
    down_w = w_down[0]
    down_cols = [down_w[:, q * col_width : (q + 1) * col_width] for q in range(n_ctx)]

    pre_gate = jnp.einsum("nsd,ndf->sf", rows_in, gate_w, preferred_element_type=jnp.float32)
    pre_up = jnp.einsum("nsd,ndf->sf", rows_in, up_w, preferred_element_type=jnp.float32)
    sigma = jax.nn.sigmoid(pre_gate)
    activated = pre_gate * sigma
    hidden = (activated * pre_up).astype(jnp.bfloat16)
    partial_out = jnp.stack(
        [jnp.dot(hidden, cols, preferred_element_type=jnp.float32) for cols in down_cols]
    ).astype(jnp.bfloat16)
    gate_part = jnp.einsum(
        "nsd,nsd->s", partial_out.astype(jnp.float32), grads_in.astype(jnp.float32)
    )
    gate_sum = all_sum(gate_part, n_ctx)

    contract_last = (((1,), (1,)), ((), ()))
    down_t = sum(
        lax.dot_general(grads_in[q], down_cols[q], contract_last, preferred_element_type=jnp.float32)
        for q in range(n_ctx)
    )
    hidden_grad = gate_column * down_t
    grad_gate = (hidden_grad * pre_up * sigma * (1.0 + pre_gate * (1.0 - sigma))).astype(
        jnp.bfloat16
    )
    grad_up = (hidden_grad * activated).astype(jnp.bfloat16)
    back_terms = jnp.einsum(
        "sf,ndf->nsd", grad_gate, gate_w, preferred_element_type=jnp.float32
    ) + jnp.einsum("sf,ndf->nsd", grad_up, up_w, preferred_element_type=jnp.float32)
    back_terms = back_terms.astype(jnp.bfloat16)
    both_parts = jnp.concatenate([partial_out, back_terms], axis=2).astype(jnp.float32)
    both_sums = scatter_sum(both_parts, n_ctx, me).astype(jnp.bfloat16)
    back = to_experts(with_cols(both_sums, gate_sum, pad))
    back_grad = back[:, col_width : 2 * col_width]

    w_gate_grad = jnp.einsum(
        "nsd,sf->ndf", rows_in, grad_gate, preferred_element_type=jnp.float32
    ).astype(jnp.bfloat16).reshape(1, n_ctx * col_width, group)
    w_up_grad = jnp.einsum(
        "nsd,sf->ndf", rows_in, grad_up, preferred_element_type=jnp.float32
    ).astype(jnp.bfloat16).reshape(1, n_ctx * col_width, group)

    slot_gg = join_f32(back[:, 2 * col_width], back[:, 2 * col_width + 1])
    out_rows = back[:, :col_width]
    layer_out = jnp.zeros((tok_rows, col_width), jnp.float32)
    input_grad = jnp.zeros((tok_rows, col_width), jnp.float32)
    gate_terms = []
    for r, chosen in enumerate(route_maps):
        pick = chosen.astype(jnp.bfloat16)
        rows_r = jnp.dot(pick, out_rows, preferred_element_type=jnp.float32)
        layer_out = layer_out + route_gates[:, r][:, None] * rows_r
        input_grad = input_grad + jnp.dot(pick, back_grad, preferred_element_type=jnp.float32)
        gate_terms.append(jnp.sum(jnp.where(chosen, slot_gg[None, :], 0.0), axis=1))
    gate_grad = jnp.stack(gate_terms, axis=1)
    return (
        layer_out.astype(jnp.bfloat16),
        input_grad.astype(jnp.bfloat16),
        gate_grad,
        w_gate_grad,
        w_up_grad,
    )


def solution(mesh):
    in_specs = (
        P("ep", "ctx"),
        P("ep", "ctx"),
        P("ep", None),
        P("ep", None),
        P("ep", None, "ctx"),
        P("ep", None, "ctx"),
        P("ep", "ctx", None),
    )
    out_specs = (
        P("ep", "ctx"),
        P("ep", "ctx"),
        P("ep", None),
        P("ep", None, "ctx"),
        P("ep", None, "ctx"),
    )
    return jax.shard_map(shards, mesh=mesh, in_specs=in_specs, out_specs=out_specs, check_vma=False)
```

```python
import jax
import jax.numpy as jnp
from jax import lax
from jax.sharding import PartitionSpec as P


def route_onehot(expert_ids, experts, capacity):
    tok_rows, routes = expert_ids.shape
    flat_ids = expert_ids.reshape(-1)
    labels = jnp.arange(experts, dtype=jnp.int32)
    onehot = (flat_ids[:, None] == labels[None, :]).astype(jnp.bfloat16)
    pairs = jnp.arange(flat_ids.shape[0], dtype=jnp.int32)
    before = (pairs[:, None] > pairs[None, :]).astype(jnp.bfloat16)
    earlier = jnp.dot(before, onehot, preferred_element_type=jnp.float32)
    slot_rank = jnp.sum(earlier * onehot.astype(jnp.float32), axis=1).astype(jnp.int32)
    slot_ids = (flat_ids * capacity + slot_rank).reshape(tok_rows, routes)
    positions = jnp.arange(experts * capacity, dtype=jnp.int32)
    return [slot_ids[:, r][:, None] == positions[None, :] for r in range(routes)]


def split_f32(values):
    hi = values.astype(jnp.bfloat16)
    lo = (values - hi.astype(jnp.float32)).astype(jnp.bfloat16)
    return hi, lo


def join_f32(hi, lo):
    return hi.astype(jnp.float32) + lo.astype(jnp.float32)


def ctx_bits(n_ctx):
    bits = n_ctx.bit_length() - 1
    assert 1 << bits == n_ctx
    return bits


def xor_pairs(n_ctx, bit):
    return [(i, i ^ (1 << bit)) for i in range(n_ctx)]


def gather_blocks(block, n_ctx, me):
    held = block[None]
    for bit in reversed(range(ctx_bits(n_ctx))):
        other = lax.ppermute(held, "ctx", xor_pairs(n_ctx, bit))
        mine_first = ((me >> bit) & 1) == 0
        pair = jnp.where(
            mine_first, jnp.stack([held, other], axis=1), jnp.stack([other, held], axis=1)
        )
        held = pair.reshape((-1,) + block.shape)
    return held


def scatter_sum(blocks, n_ctx, me):
    acc = blocks
    for bit in range(ctx_bits(n_ctx)):
        halves = acc.reshape((-1, 2) + acc.shape[1:])
        keep_first = ((me >> bit) & 1) == 0
        keep = jnp.where(keep_first, halves[:, 0], halves[:, 1])
        send = jnp.where(keep_first, halves[:, 1], halves[:, 0]).astype(jnp.bfloat16)
        got = lax.ppermute(send, "ctx", xor_pairs(n_ctx, bit))
        acc = keep + got.astype(jnp.float32)
    return acc[0]


def all_sum(values, n_ctx):
    for bit in range(ctx_bits(n_ctx)):
        values = values + lax.ppermute(values, "ctx", xor_pairs(n_ctx, bit))
    return values


def with_cols(rows, values, pad):
    hi, lo = split_f32(values)
    lane = lax.broadcasted_iota(jnp.int32, (rows.shape[0], pad), 1)
    zero = jnp.zeros((), jnp.bfloat16)
    cols = jnp.where(lane == 0, hi[:, None], jnp.where(lane == 1, lo[:, None], zero))
    return jnp.concatenate([rows, cols], axis=1)


def shards(tokens, cotangent, expert_ids, route_gates, w_gate, w_up, w_down):
    tok_rows, routes = expert_ids.shape
    experts = lax.axis_size("ep")
    n_ctx = lax.axis_size("ctx")
    me = lax.axis_index("ctx")
    capacity = 3 * tok_rows * routes // (2 * experts)
    slot_count = experts * capacity
    col_width = tokens.shape[1]
    pad = 128
    route_maps = route_onehot(expert_ids, experts, capacity)

    def place(values):
        placed = jnp.zeros((slot_count, values.shape[1]), jnp.float32)
        for chosen in route_maps:
            placed = placed + jnp.einsum(
                "ts,tc->sc", chosen.astype(jnp.bfloat16), values, preferred_element_type=jnp.float32
            )
        return placed.astype(jnp.bfloat16)

    def to_experts(rows):
        sent = rows.reshape(experts, capacity, rows.shape[1])
        got = lax.all_to_all(sent, "ep", split_axis=0, concat_axis=0, tiled=True)
        return got.reshape(slot_count, rows.shape[1])

    slot_gates = jnp.zeros((slot_count,), jnp.float32)
    for r, chosen in enumerate(route_maps):
        slot_gates = slot_gates + jnp.sum(jnp.where(chosen, route_gates[:, r][:, None], 0.0), axis=0)
    got_x = to_experts(with_cols(place(tokens), slot_gates, pad))
    gate_column = join_f32(got_x[:, col_width], got_x[:, col_width + 1])[:, None]
    rows_in = gather_blocks(got_x[:, :col_width], n_ctx, me)
    got_dy = to_experts(place(cotangent))
    grads_in = gather_blocks(got_dy, n_ctx, me)

    group = w_gate.shape[2]
    gate_w = w_gate[0].reshape(n_ctx, col_width, group)
    up_w = w_up[0].reshape(n_ctx, col_width, group)
    down_w = w_down[0]
    down_cols = [down_w[:, q * col_width : (q + 1) * col_width] for q in range(n_ctx)]

    pre_gate = jnp.einsum("nsd,ndf->sf", rows_in, gate_w, preferred_element_type=jnp.float32)
    pre_up = jnp.einsum("nsd,ndf->sf", rows_in, up_w, preferred_element_type=jnp.float32)
    sigma = jax.nn.sigmoid(pre_gate)
    activated = pre_gate * sigma
    hidden = (activated * pre_up).astype(jnp.bfloat16)
    partial_out = jnp.stack(
        [jnp.dot(hidden, cols, preferred_element_type=jnp.float32) for cols in down_cols]
    ).astype(jnp.bfloat16)
    gate_part = jnp.einsum(
        "nsd,nsd->s", partial_out.astype(jnp.float32), grads_in.astype(jnp.float32)
    )
    expert_out = scatter_sum(partial_out.astype(jnp.float32), n_ctx, me).astype(jnp.bfloat16)
    gate_sum = all_sum(gate_part, n_ctx)
    back_out = to_experts(with_cols(expert_out, gate_sum, pad))

    contract_last = (((1,), (1,)), ((), ()))
    down_t = sum(
        lax.dot_general(grads_in[q], down_cols[q], contract_last, preferred_element_type=jnp.float32)
        for q in range(n_ctx)
    )
    hidden_grad = gate_column * down_t
    grad_gate = (hidden_grad * pre_up * sigma * (1.0 + pre_gate * (1.0 - sigma))).astype(
        jnp.bfloat16
    )
    grad_up = (hidden_grad * activated).astype(jnp.bfloat16)
    back_terms = jnp.einsum(
        "sf,ndf->nsd", grad_gate, gate_w, preferred_element_type=jnp.float32
    ) + jnp.einsum("sf,ndf->nsd", grad_up, up_w, preferred_element_type=jnp.float32)
    back_terms = back_terms.astype(jnp.bfloat16).astype(jnp.float32)
    slot_grad = scatter_sum(back_terms, n_ctx, me).astype(jnp.bfloat16)
    back_grad = to_experts(slot_grad)

    w_gate_grad = jnp.einsum(
        "nsd,sf->ndf", rows_in, grad_gate, preferred_element_type=jnp.float32
    ).astype(jnp.bfloat16).reshape(1, n_ctx * col_width, group)
    w_up_grad = jnp.einsum(
        "nsd,sf->ndf", rows_in, grad_up, preferred_element_type=jnp.float32
    ).astype(jnp.bfloat16).reshape(1, n_ctx * col_width, group)

    slot_gg = join_f32(back_out[:, col_width], back_out[:, col_width + 1])
    out_rows = back_out[:, :col_width]
    layer_out = jnp.zeros((tok_rows, col_width), jnp.float32)
    input_grad = jnp.zeros((tok_rows, col_width), jnp.float32)
    gate_terms = []
    for r, chosen in enumerate(route_maps):
        pick = chosen.astype(jnp.bfloat16)
        rows_r = jnp.dot(pick, out_rows, preferred_element_type=jnp.float32)
        layer_out = layer_out + route_gates[:, r][:, None] * rows_r
        input_grad = input_grad + jnp.dot(pick, back_grad, preferred_element_type=jnp.float32)
        gate_terms.append(jnp.sum(jnp.where(chosen, slot_gg[None, :], 0.0), axis=1))
    gate_grad = jnp.stack(gate_terms, axis=1)
    return (
        layer_out.astype(jnp.bfloat16),
        input_grad.astype(jnp.bfloat16),
        gate_grad,
        w_gate_grad,
        w_up_grad,
    )


def solution(mesh):
    in_specs = (
        P("ep", "ctx"),
        P("ep", "ctx"),
        P("ep", None),
        P("ep", None),
        P("ep", None, "ctx"),
        P("ep", None, "ctx"),
        P("ep", "ctx", None),
    )
    out_specs = (
        P("ep", "ctx"),
        P("ep", "ctx"),
        P("ep", None),
        P("ep", None, "ctx"),
        P("ep", None, "ctx"),
    )
    return jax.shard_map(shards, mesh=mesh, in_specs=in_specs, out_specs=out_specs, check_vma=False)
```

```python
import jax
import jax.numpy as jnp
from jax import lax
from jax.sharding import PartitionSpec as P


def route_onehot(expert_ids, experts, capacity):
    tok_rows, routes = expert_ids.shape
    flat_ids = expert_ids.reshape(-1)
    labels = jnp.arange(experts, dtype=jnp.int32)
    onehot = (flat_ids[:, None] == labels[None, :]).astype(jnp.bfloat16)
    pairs = jnp.arange(flat_ids.shape[0], dtype=jnp.int32)
    before = (pairs[:, None] > pairs[None, :]).astype(jnp.bfloat16)
    earlier = jnp.dot(before, onehot, preferred_element_type=jnp.float32)
    slot_rank = jnp.sum(earlier * onehot.astype(jnp.float32), axis=1).astype(jnp.int32)
    slot_ids = (flat_ids * capacity + slot_rank).reshape(tok_rows, routes)
    positions = jnp.arange(experts * capacity, dtype=jnp.int32)
    return [slot_ids[:, r][:, None] == positions[None, :] for r in range(routes)]


def split_f32(values):
    hi = values.astype(jnp.bfloat16)
    lo = (values - hi.astype(jnp.float32)).astype(jnp.bfloat16)
    return hi, lo


def join_f32(hi, lo):
    return hi.astype(jnp.float32) + lo.astype(jnp.float32)


def ctx_bits(n_ctx):
    bits = n_ctx.bit_length() - 1
    assert 1 << bits == n_ctx
    return bits


def xor_pairs(n_ctx, bit):
    return [(i, i ^ (1 << bit)) for i in range(n_ctx)]


def gather_blocks(block, n_ctx, me):
    held = block[None]
    for bit in reversed(range(ctx_bits(n_ctx))):
        other = lax.ppermute(held, "ctx", xor_pairs(n_ctx, bit))
        mine_first = ((me >> bit) & 1) == 0
        pair = jnp.where(
            mine_first, jnp.stack([held, other], axis=1), jnp.stack([other, held], axis=1)
        )
        held = pair.reshape((-1,) + block.shape)
    return held


def after(values, needed):
    zero = needed[(0,) * needed.ndim].astype(jnp.float32) * 0.0
    return values + zero.astype(values.dtype)


def scatter_sum(blocks, n_ctx, me, wait_for=None):
    acc = blocks
    for bit in range(ctx_bits(n_ctx)):
        halves = acc.reshape((-1, 2) + acc.shape[1:])
        keep_first = ((me >> bit) & 1) == 0
        keep = jnp.where(keep_first, halves[:, 0], halves[:, 1])
        send = jnp.where(keep_first, halves[:, 1], halves[:, 0]).astype(jnp.bfloat16)
        if bit == 1 and wait_for is not None:
            send = after(send, wait_for)
        got = lax.ppermute(send, "ctx", xor_pairs(n_ctx, bit))
        acc = keep + got.astype(jnp.float32)
    return acc[0]


def all_sum(values, n_ctx):
    for bit in range(ctx_bits(n_ctx)):
        values = values + lax.ppermute(values, "ctx", xor_pairs(n_ctx, bit))
    return values


def with_cols(rows, values, pad):
    hi, lo = split_f32(values)
    zeros = jnp.zeros((rows.shape[0], pad - 2), jnp.bfloat16)
    return jnp.concatenate([rows, hi[:, None], lo[:, None], zeros], axis=1)


def shards(tokens, cotangent, expert_ids, route_gates, w_gate, w_up, w_down):
    tok_rows, routes = expert_ids.shape
    experts = lax.axis_size("ep")
    n_ctx = lax.axis_size("ctx")
    me = lax.axis_index("ctx")
    capacity = 3 * tok_rows * routes // (2 * experts)
    slot_count = experts * capacity
    col_width = tokens.shape[1]
    pad = 128
    route_maps = route_onehot(expert_ids, experts, capacity)

    def place(values):
        placed = jnp.zeros((slot_count, values.shape[1]), jnp.float32)
        for chosen in route_maps:
            placed = placed + jnp.einsum(
                "ts,tc->sc", chosen.astype(jnp.bfloat16), values, preferred_element_type=jnp.float32
            )
        return placed.astype(jnp.bfloat16)

    def to_experts(rows):
        sent = rows.reshape(experts, capacity, rows.shape[1])
        got = lax.all_to_all(sent, "ep", split_axis=0, concat_axis=0, tiled=True)
        return got.reshape(slot_count, rows.shape[1])

    slot_gates = jnp.zeros((slot_count,), jnp.float32)
    for r, chosen in enumerate(route_maps):
        slot_gates = slot_gates + jnp.sum(jnp.where(chosen, route_gates[:, r][:, None], 0.0), axis=0)
    got_x = to_experts(with_cols(place(tokens), slot_gates, pad))
    gate_column = join_f32(got_x[:, col_width], got_x[:, col_width + 1])[:, None]
    rows_in = gather_blocks(got_x[:, :col_width], n_ctx, me)
    got_dy = to_experts(place(cotangent))
    grads_in = gather_blocks(got_dy, n_ctx, me)

    group = w_gate.shape[2]
    gate_w = w_gate[0].reshape(n_ctx, col_width, group)
    up_w = w_up[0].reshape(n_ctx, col_width, group)
    down_w = w_down[0]
    down_cols = [down_w[:, q * col_width : (q + 1) * col_width] for q in range(n_ctx)]

    pre_gate = jnp.einsum("nsd,ndf->sf", rows_in, gate_w, preferred_element_type=jnp.float32)
    pre_up = jnp.einsum("nsd,ndf->sf", rows_in, up_w, preferred_element_type=jnp.float32)
    sigma = jax.nn.sigmoid(pre_gate)
    activated = pre_gate * sigma
    hidden = (activated * pre_up).astype(jnp.bfloat16)
    partial_out = jnp.stack(
        [jnp.dot(hidden, cols, preferred_element_type=jnp.float32) for cols in down_cols]
    ).astype(jnp.bfloat16)
    gate_part = jnp.einsum(
        "nsd,nsd->s", partial_out.astype(jnp.float32), grads_in.astype(jnp.float32)
    )
    gate_sum = all_sum(gate_part, n_ctx)

    contract_last = (((1,), (1,)), ((), ()))
    down_t = sum(
        lax.dot_general(grads_in[q], down_cols[q], contract_last, preferred_element_type=jnp.float32)
        for q in range(n_ctx)
    )
    hidden_grad = gate_column * down_t
    grad_gate = (hidden_grad * pre_up * sigma * (1.0 + pre_gate * (1.0 - sigma))).astype(
        jnp.bfloat16
    )
    grad_up = (hidden_grad * activated).astype(jnp.bfloat16)
    back_terms = jnp.einsum(
        "sf,ndf->nsd", grad_gate, gate_w, preferred_element_type=jnp.float32
    ) + jnp.einsum("sf,ndf->nsd", grad_up, up_w, preferred_element_type=jnp.float32)
    back_terms = back_terms.astype(jnp.bfloat16).astype(jnp.float32)
    slot_grad = scatter_sum(back_terms, n_ctx, me).astype(jnp.bfloat16)
    back_grad = to_experts(slot_grad)
    expert_out = scatter_sum(
        partial_out.astype(jnp.float32), n_ctx, me, slot_grad
    ).astype(jnp.bfloat16)
    back_out = to_experts(with_cols(expert_out, gate_sum, pad))

    w_gate_grad = jnp.einsum(
        "nsd,sf->ndf", rows_in, grad_gate, preferred_element_type=jnp.float32
    ).astype(jnp.bfloat16).reshape(1, n_ctx * col_width, group)
    w_up_grad = jnp.einsum(
        "nsd,sf->ndf", rows_in, grad_up, preferred_element_type=jnp.float32
    ).astype(jnp.bfloat16).reshape(1, n_ctx * col_width, group)

    slot_gg = join_f32(back_out[:, col_width], back_out[:, col_width + 1])
    out_rows = back_out[:, :col_width]
    layer_out = jnp.zeros((tok_rows, col_width), jnp.float32)
    input_grad = jnp.zeros((tok_rows, col_width), jnp.float32)
    gate_terms = []
    for r, chosen in enumerate(route_maps):
        pick = chosen.astype(jnp.bfloat16)
        rows_r = jnp.dot(pick, out_rows, preferred_element_type=jnp.float32)
        layer_out = layer_out + route_gates[:, r][:, None] * rows_r
        input_grad = input_grad + jnp.dot(pick, back_grad, preferred_element_type=jnp.float32)
        gate_terms.append(jnp.sum(jnp.where(chosen, slot_gg[None, :], 0.0), axis=1))
    gate_grad = jnp.stack(gate_terms, axis=1)
    return (
        layer_out.astype(jnp.bfloat16),
        input_grad.astype(jnp.bfloat16),
        gate_grad,
        w_gate_grad,
        w_up_grad,
    )


def solution(mesh):
    in_specs = (
        P("ep", "ctx"),
        P("ep", "ctx"),
        P("ep", None),
        P("ep", None),
        P("ep", None, "ctx"),
        P("ep", None, "ctx"),
        P("ep", "ctx", None),
    )
    out_specs = (
        P("ep", "ctx"),
        P("ep", "ctx"),
        P("ep", None),
        P("ep", None, "ctx"),
        P("ep", None, "ctx"),
    )
    return jax.shard_map(shards, mesh=mesh, in_specs=in_specs, out_specs=out_specs, check_vma=False)
```

```python
import jax
import jax.numpy as jnp
from jax import lax
from jax.sharding import PartitionSpec as P


def route_onehot(expert_ids, experts, capacity):
    tok_rows, routes = expert_ids.shape
    flat_ids = expert_ids.reshape(-1)
    labels = jnp.arange(experts, dtype=jnp.int32)
    onehot = (flat_ids[:, None] == labels[None, :]).astype(jnp.bfloat16)
    pairs = jnp.arange(flat_ids.shape[0], dtype=jnp.int32)
    before = (pairs[:, None] > pairs[None, :]).astype(jnp.bfloat16)
    earlier = jnp.dot(before, onehot, preferred_element_type=jnp.float32)
    slot_rank = jnp.sum(earlier * onehot.astype(jnp.float32), axis=1).astype(jnp.int32)
    slot_ids = (flat_ids * capacity + slot_rank).reshape(tok_rows, routes)
    positions = jnp.arange(experts * capacity, dtype=jnp.int32)
    return [slot_ids[:, r][:, None] == positions[None, :] for r in range(routes)]


def split_f32(values):
    hi = values.astype(jnp.bfloat16)
    lo = (values - hi.astype(jnp.float32)).astype(jnp.bfloat16)
    return hi, lo


def join_f32(hi, lo):
    return hi.astype(jnp.float32) + lo.astype(jnp.float32)


def ctx_bits(n_ctx):
    bits = n_ctx.bit_length() - 1
    assert 1 << bits == n_ctx
    return bits


def xor_pairs(n_ctx, bit):
    return [(i, i ^ (1 << bit)) for i in range(n_ctx)]


def gather_blocks(block, n_ctx, me):
    held = block[None]
    for bit in reversed(range(ctx_bits(n_ctx))):
        other = lax.ppermute(held, "ctx", xor_pairs(n_ctx, bit))
        mine_first = ((me >> bit) & 1) == 0
        pair = jnp.where(
            mine_first, jnp.stack([held, other], axis=1), jnp.stack([other, held], axis=1)
        )
        held = pair.reshape((-1,) + block.shape)
    return held


def scatter_sum(blocks, n_ctx, me):
    acc = blocks
    for bit in range(ctx_bits(n_ctx)):
        halves = acc.reshape((-1, 2) + acc.shape[1:])
        keep_first = ((me >> bit) & 1) == 0
        keep = jnp.where(keep_first, halves[:, 0], halves[:, 1])
        send = jnp.where(keep_first, halves[:, 1], halves[:, 0]).astype(jnp.bfloat16)
        got = lax.ppermute(send, "ctx", xor_pairs(n_ctx, bit))
        acc = keep + got.astype(jnp.float32)
    return acc[0]


def all_sum(values, n_ctx):
    for bit in range(ctx_bits(n_ctx)):
        values = values + lax.ppermute(values, "ctx", xor_pairs(n_ctx, bit))
    return values


def with_cols(rows, values, pad):
    hi, lo = split_f32(values)
    zeros = jnp.zeros((rows.shape[0], pad - 2), jnp.bfloat16)
    return jnp.concatenate([rows, hi[:, None], lo[:, None], zeros], axis=1)


def shards(tokens, cotangent, expert_ids, route_gates, w_gate, w_up, w_down):
    tok_rows, routes = expert_ids.shape
    experts = lax.axis_size("ep")
    n_ctx = lax.axis_size("ctx")
    me = lax.axis_index("ctx")
    capacity = 3 * tok_rows * routes // (2 * experts)
    slot_count = experts * capacity
    col_width = tokens.shape[1]
    pad = 128
    route_maps = route_onehot(expert_ids, experts, capacity)

    def place(values):
        placed = jnp.zeros((slot_count, values.shape[1]), jnp.float32)
        for chosen in route_maps:
            placed = placed + jnp.einsum(
                "ts,tc->sc", chosen.astype(jnp.bfloat16), values, preferred_element_type=jnp.float32
            )
        return placed.astype(jnp.bfloat16)

    def to_experts(rows):
        sent = rows.reshape(experts, capacity, rows.shape[1])
        got = lax.all_to_all(sent, "ep", split_axis=0, concat_axis=0, tiled=True)
        return got.reshape(slot_count, rows.shape[1])

    slot_gates = jnp.zeros((slot_count,), jnp.float32)
    for r, chosen in enumerate(route_maps):
        slot_gates = slot_gates + jnp.sum(jnp.where(chosen, route_gates[:, r][:, None], 0.0), axis=0)
    got_x = to_experts(with_cols(place(tokens), slot_gates, pad))
    gate_column = join_f32(got_x[:, col_width], got_x[:, col_width + 1])[:, None]
    rows_in = gather_blocks(got_x[:, :col_width], n_ctx, me)
    got_dy = to_experts(place(cotangent))
    grads_in = gather_blocks(got_dy, n_ctx, me)

    group = w_gate.shape[2]
    gate_w = w_gate[0].reshape(n_ctx, col_width, group)
    up_w = w_up[0].reshape(n_ctx, col_width, group)
    down_w = w_down[0]
    down_cols = [down_w[:, q * col_width : (q + 1) * col_width] for q in range(n_ctx)]

    pre_gate = jnp.einsum("nsd,ndf->sf", rows_in, gate_w, preferred_element_type=jnp.float32)
    pre_up = jnp.einsum("nsd,ndf->sf", rows_in, up_w, preferred_element_type=jnp.float32)
    sigma = jax.nn.sigmoid(pre_gate)
    activated = pre_gate * sigma
    hidden = (activated * pre_up).astype(jnp.bfloat16)
    partial_out = jnp.stack(
        [jnp.dot(hidden, cols, preferred_element_type=jnp.float32) for cols in down_cols]
    ).astype(jnp.bfloat16)
    gate_part = jnp.einsum(
        "nsd,nsd->s", partial_out.astype(jnp.float32), grads_in.astype(jnp.float32)
    )
    gate_cols = with_cols(jnp.zeros((slot_count, 0), jnp.bfloat16), gate_part, pad)
    out_parts = jnp.concatenate(
        [partial_out, jnp.broadcast_to(gate_cols[None], (n_ctx, slot_count, pad))], axis=2
    )
    out_sums = scatter_sum(out_parts.astype(jnp.float32), n_ctx, me)
    expert_out = out_sums[:, :col_width].astype(jnp.bfloat16)
    gate_sum = out_sums[:, col_width] + out_sums[:, col_width + 1]
    back_out = to_experts(with_cols(expert_out, gate_sum, pad))

    contract_last = (((1,), (1,)), ((), ()))
    down_t = sum(
        lax.dot_general(grads_in[q], down_cols[q], contract_last, preferred_element_type=jnp.float32)
        for q in range(n_ctx)
    )
    hidden_grad = gate_column * down_t
    grad_gate = (hidden_grad * pre_up * sigma * (1.0 + pre_gate * (1.0 - sigma))).astype(
        jnp.bfloat16
    )
    grad_up = (hidden_grad * activated).astype(jnp.bfloat16)
    back_terms = jnp.einsum(
        "sf,ndf->nsd", grad_gate, gate_w, preferred_element_type=jnp.float32
    ) + jnp.einsum("sf,ndf->nsd", grad_up, up_w, preferred_element_type=jnp.float32)
    back_terms = back_terms.astype(jnp.bfloat16).astype(jnp.float32)
    slot_grad = scatter_sum(back_terms, n_ctx, me).astype(jnp.bfloat16)
    back_grad = to_experts(slot_grad)

    w_gate_grad = jnp.einsum(
        "nsd,sf->ndf", rows_in, grad_gate, preferred_element_type=jnp.float32
    ).astype(jnp.bfloat16).reshape(1, n_ctx * col_width, group)
    w_up_grad = jnp.einsum(
        "nsd,sf->ndf", rows_in, grad_up, preferred_element_type=jnp.float32
    ).astype(jnp.bfloat16).reshape(1, n_ctx * col_width, group)

    slot_gg = join_f32(back_out[:, col_width], back_out[:, col_width + 1])
    out_rows = back_out[:, :col_width]
    layer_out = jnp.zeros((tok_rows, col_width), jnp.float32)
    input_grad = jnp.zeros((tok_rows, col_width), jnp.float32)
    gate_terms = []
    for r, chosen in enumerate(route_maps):
        pick = chosen.astype(jnp.bfloat16)
        rows_r = jnp.dot(pick, out_rows, preferred_element_type=jnp.float32)
        layer_out = layer_out + route_gates[:, r][:, None] * rows_r
        input_grad = input_grad + jnp.dot(pick, back_grad, preferred_element_type=jnp.float32)
        gate_terms.append(jnp.sum(jnp.where(chosen, slot_gg[None, :], 0.0), axis=1))
    gate_grad = jnp.stack(gate_terms, axis=1)
    return (
        layer_out.astype(jnp.bfloat16),
        input_grad.astype(jnp.bfloat16),
        gate_grad,
        w_gate_grad,
        w_up_grad,
    )


def solution(mesh):
    in_specs = (
        P("ep", "ctx"),
        P("ep", "ctx"),
        P("ep", None),
        P("ep", None),
        P("ep", None, "ctx"),
        P("ep", None, "ctx"),
        P("ep", "ctx", None),
    )
    out_specs = (
        P("ep", "ctx"),
        P("ep", "ctx"),
        P("ep", None),
        P("ep", None, "ctx"),
        P("ep", None, "ctx"),
    )
    return jax.shard_map(shards, mesh=mesh, in_specs=in_specs, out_specs=out_specs, check_vma=False)
```

```python
import jax
import jax.numpy as jnp
from jax import lax
from jax.sharding import PartitionSpec as P


def route_onehot(expert_ids, experts, capacity):
    tok_rows, routes = expert_ids.shape
    flat_ids = expert_ids.reshape(-1)
    labels = jnp.arange(experts, dtype=jnp.int32)
    onehot = (flat_ids[:, None] == labels[None, :]).astype(jnp.bfloat16)
    pairs = jnp.arange(flat_ids.shape[0], dtype=jnp.int32)
    before = (pairs[:, None] > pairs[None, :]).astype(jnp.bfloat16)
    earlier = jnp.dot(before, onehot, preferred_element_type=jnp.float32)
    slot_rank = jnp.sum(earlier * onehot.astype(jnp.float32), axis=1).astype(jnp.int32)
    slot_ids = (flat_ids * capacity + slot_rank).reshape(tok_rows, routes)
    positions = jnp.arange(experts * capacity, dtype=jnp.int32)
    return [slot_ids[:, r][:, None] == positions[None, :] for r in range(routes)]


def split_f32(values):
    hi = values.astype(jnp.bfloat16)
    lo = (values - hi.astype(jnp.float32)).astype(jnp.bfloat16)
    return hi, lo


def join_f32(hi, lo):
    return hi.astype(jnp.float32) + lo.astype(jnp.float32)


def ctx_bits(n_ctx):
    bits = n_ctx.bit_length() - 1
    assert 1 << bits == n_ctx
    return bits


def xor_pairs(n_ctx, bit):
    return [(i, i ^ (1 << bit)) for i in range(n_ctx)]


def gather_blocks(block, n_ctx, me):
    held = block[None]
    for bit in reversed(range(ctx_bits(n_ctx))):
        other = lax.ppermute(held, "ctx", xor_pairs(n_ctx, bit))
        mine_first = ((me >> bit) & 1) == 0
        pair = jnp.where(
            mine_first, jnp.stack([held, other], axis=1), jnp.stack([other, held], axis=1)
        )
        held = pair.reshape((-1,) + block.shape)
    return held


def scatter_sum(blocks, n_ctx, me):
    acc = blocks
    for bit in range(ctx_bits(n_ctx)):
        halves = acc.reshape((-1, 2) + acc.shape[1:])
        keep_first = ((me >> bit) & 1) == 0
        keep = jnp.where(keep_first, halves[:, 0], halves[:, 1])
        send = jnp.where(keep_first, halves[:, 1], halves[:, 0]).astype(jnp.bfloat16)
        got = lax.ppermute(send, "ctx", xor_pairs(n_ctx, bit))
        acc = keep + got.astype(jnp.float32)
    return acc[0]


def all_sum(values, n_ctx):
    for bit in range(ctx_bits(n_ctx)):
        values = values + lax.ppermute(values, "ctx", xor_pairs(n_ctx, bit))
    return values


def with_cols(rows, values, pad):
    hi, lo = split_f32(values)
    zeros = jnp.zeros((rows.shape[0], pad - 2), jnp.bfloat16)
    return jnp.concatenate([rows, hi[:, None], lo[:, None], zeros], axis=1)


def shards(tokens, cotangent, expert_ids, route_gates, w_gate, w_up, w_down):
    tok_rows, routes = expert_ids.shape
    experts = lax.axis_size("ep")
    n_ctx = lax.axis_size("ctx")
    me = lax.axis_index("ctx")
    capacity = 3 * tok_rows * routes // (2 * experts)
    slot_count = experts * capacity
    col_width = tokens.shape[1]
    pad = 128
    route_maps = route_onehot(expert_ids, experts, capacity)

    def place(values):
        placed = jnp.zeros((slot_count, values.shape[1]), jnp.float32)
        for chosen in route_maps:
            placed = placed + jnp.einsum(
                "ts,tc->sc", chosen.astype(jnp.bfloat16), values, preferred_element_type=jnp.float32
            )
        return placed.astype(jnp.bfloat16)

    def to_experts(rows):
        sent = rows.reshape(experts, capacity, rows.shape[1])
        got = lax.all_to_all(sent, "ep", split_axis=0, concat_axis=0, tiled=True)
        return got.reshape(slot_count, rows.shape[1])

    slot_gates = jnp.zeros((slot_count,), jnp.float32)
    for r, chosen in enumerate(route_maps):
        slot_gates = slot_gates + jnp.sum(jnp.where(chosen, route_gates[:, r][:, None], 0.0), axis=0)
    got_x = to_experts(with_cols(place(tokens), slot_gates, pad))
    gate_column = join_f32(got_x[:, col_width], got_x[:, col_width + 1])[:, None]
    rows_in = gather_blocks(got_x[:, :col_width], n_ctx, me)
    got_dy = to_experts(place(cotangent))
    grads_in = gather_blocks(got_dy, n_ctx, me)

    group = w_gate.shape[2]
    gate_w = w_gate[0].reshape(n_ctx, col_width, group)
    up_w = w_up[0].reshape(n_ctx, col_width, group)
    down_w = w_down[0]
    down_cols = [down_w[:, q * col_width : (q + 1) * col_width] for q in range(n_ctx)]

    pre_gate = jnp.einsum("nsd,ndf->sf", rows_in, gate_w, preferred_element_type=jnp.float32)
    pre_up = jnp.einsum("nsd,ndf->sf", rows_in, up_w, preferred_element_type=jnp.float32)
    sigma = jax.nn.sigmoid(pre_gate)
    activated = pre_gate * sigma
    hidden = (activated * pre_up).astype(jnp.bfloat16)
    partial_out = jnp.stack(
        [jnp.dot(hidden, cols, preferred_element_type=jnp.float32) for cols in down_cols]
    ).astype(jnp.bfloat16)
    gate_part = jnp.einsum(
        "nsd,nsd->s", partial_out.astype(jnp.float32), grads_in.astype(jnp.float32)
    )
    expert_out = scatter_sum(partial_out.astype(jnp.float32), n_ctx, me).astype(jnp.bfloat16)
    gate_sum = all_sum(gate_part, n_ctx)
    back_out = to_experts(with_cols(expert_out, gate_sum, pad))

    contract_last = (((1,), (1,)), ((), ()))
    down_t = sum(
        lax.dot_general(grads_in[q], down_cols[q], contract_last, preferred_element_type=jnp.float32)
        for q in range(n_ctx)
    )
    hidden_grad = gate_column * down_t
    grad_gate = (hidden_grad * pre_up * sigma * (1.0 + pre_gate * (1.0 - sigma))).astype(
        jnp.bfloat16
    )
    grad_up = (hidden_grad * activated).astype(jnp.bfloat16)
    back_terms = jnp.einsum(
        "sf,ndf->nsd", grad_gate, gate_w, preferred_element_type=jnp.float32
    ) + jnp.einsum("sf,ndf->nsd", grad_up, up_w, preferred_element_type=jnp.float32)
    back_terms = back_terms.astype(jnp.bfloat16).astype(jnp.float32)
    slot_grad = scatter_sum(back_terms, n_ctx, me).astype(jnp.bfloat16)
    back_grad = to_experts(slot_grad)

    w_gate_grad = jnp.einsum(
        "nsd,sf->ndf", rows_in, grad_gate, preferred_element_type=jnp.float32
    ).astype(jnp.bfloat16).reshape(1, n_ctx * col_width, group)
    w_up_grad = jnp.einsum(
        "nsd,sf->ndf", rows_in, grad_up, preferred_element_type=jnp.float32
    ).astype(jnp.bfloat16).reshape(1, n_ctx * col_width, group)

    layer_out = jnp.zeros((tok_rows, col_width), jnp.float32)
    input_grad = jnp.zeros((tok_rows, col_width), jnp.float32)
    gate_terms = []
    for r, chosen in enumerate(route_maps):
        pick = chosen.astype(jnp.bfloat16)
        rows_r = jnp.dot(pick, back_out, preferred_element_type=jnp.float32)
        layer_out = layer_out + route_gates[:, r][:, None] * rows_r[:, :col_width]
        input_grad = input_grad + jnp.dot(pick, back_grad, preferred_element_type=jnp.float32)
        gate_terms.append(rows_r[:, col_width] + rows_r[:, col_width + 1])
    gate_grad = jnp.stack(gate_terms, axis=1)
    return (
        layer_out.astype(jnp.bfloat16),
        input_grad.astype(jnp.bfloat16),
        gate_grad,
        w_gate_grad,
        w_up_grad,
    )


def solution(mesh):
    in_specs = (
        P("ep", "ctx"),
        P("ep", "ctx"),
        P("ep", None),
        P("ep", None),
        P("ep", None, "ctx"),
        P("ep", None, "ctx"),
        P("ep", "ctx", None),
    )
    out_specs = (
        P("ep", "ctx"),
        P("ep", "ctx"),
        P("ep", None),
        P("ep", None, "ctx"),
        P("ep", None, "ctx"),
    )
    return jax.shard_map(shards, mesh=mesh, in_specs=in_specs, out_specs=out_specs, check_vma=False)
```

```python
import jax
import jax.numpy as jnp
from jax import lax
from jax.sharding import PartitionSpec as P


def route_onehot(expert_ids, experts, capacity):
    tok_rows, routes = expert_ids.shape
    flat_ids = expert_ids.reshape(-1)
    labels = jnp.arange(experts, dtype=jnp.int32)
    onehot = (flat_ids[:, None] == labels[None, :]).astype(jnp.bfloat16)
    pairs = jnp.arange(flat_ids.shape[0], dtype=jnp.int32)
    before = (pairs[:, None] > pairs[None, :]).astype(jnp.bfloat16)
    earlier = jnp.dot(before, onehot, preferred_element_type=jnp.float32)
    slot_rank = jnp.sum(earlier * onehot.astype(jnp.float32), axis=1).astype(jnp.int32)
    slot_ids = (flat_ids * capacity + slot_rank).reshape(tok_rows, routes)
    positions = jnp.arange(experts * capacity, dtype=jnp.int32)
    return [slot_ids[:, r][:, None] == positions[None, :] for r in range(routes)]


def split_f32(values):
    hi = values.astype(jnp.bfloat16)
    lo = (values - hi.astype(jnp.float32)).astype(jnp.bfloat16)
    return hi, lo


def join_f32(hi, lo):
    return hi.astype(jnp.float32) + lo.astype(jnp.float32)


def ctx_bits(n_ctx):
    bits = n_ctx.bit_length() - 1
    assert 1 << bits == n_ctx
    return bits


def xor_pairs(n_ctx, bit):
    return [(i, i ^ (1 << bit)) for i in range(n_ctx)]


def gather_blocks(block, n_ctx, me):
    held = block[None]
    for bit in reversed(range(ctx_bits(n_ctx))):
        other = lax.ppermute(held, "ctx", xor_pairs(n_ctx, bit))
        mine_first = ((me >> bit) & 1) == 0
        pair = jnp.where(
            mine_first, jnp.stack([held, other], axis=1), jnp.stack([other, held], axis=1)
        )
        held = pair.reshape((-1,) + block.shape)
    return held


def scatter_sum(blocks, n_ctx, me):
    acc = blocks
    for bit in range(ctx_bits(n_ctx)):
        halves = acc.reshape((-1, 2) + acc.shape[1:])
        keep_first = ((me >> bit) & 1) == 0
        keep = jnp.where(keep_first, halves[:, 0], halves[:, 1])
        send = jnp.where(keep_first, halves[:, 1], halves[:, 0]).astype(jnp.bfloat16)
        got = lax.ppermute(send, "ctx", xor_pairs(n_ctx, bit))
        acc = keep + got.astype(jnp.float32)
    return acc[0]


def with_cols(rows, values, pad):
    hi, lo = split_f32(values)
    zeros = jnp.zeros((rows.shape[0], pad - 2), jnp.bfloat16)
    return jnp.concatenate([rows, hi[:, None], lo[:, None], zeros], axis=1)


def shards(tokens, cotangent, expert_ids, route_gates, w_gate, w_up, w_down):
    tok_rows, routes = expert_ids.shape
    experts = lax.axis_size("ep")
    n_ctx = lax.axis_size("ctx")
    me = lax.axis_index("ctx")
    capacity = 3 * tok_rows * routes // (2 * experts)
    slot_count = experts * capacity
    col_width = tokens.shape[1]
    pad = 128
    route_maps = route_onehot(expert_ids, experts, capacity)

    def place(values):
        placed = jnp.zeros((slot_count, values.shape[1]), jnp.float32)
        for chosen in route_maps:
            placed = placed + jnp.einsum(
                "ts,tc->sc", chosen.astype(jnp.bfloat16), values, preferred_element_type=jnp.float32
            )
        return placed.astype(jnp.bfloat16)

    def to_experts(rows):
        sent = rows.reshape(experts, capacity, rows.shape[1])
        got = lax.all_to_all(sent, "ep", split_axis=0, concat_axis=0, tiled=True)
        return got.reshape(slot_count, rows.shape[1])

    slot_gates = jnp.zeros((slot_count,), jnp.float32)
    for r, chosen in enumerate(route_maps):
        slot_gates = slot_gates + jnp.sum(jnp.where(chosen, route_gates[:, r][:, None], 0.0), axis=0)
    got_x = to_experts(with_cols(place(tokens), slot_gates, pad))
    gate_column = join_f32(got_x[:, col_width], got_x[:, col_width + 1])[:, None]
    rows_in = gather_blocks(got_x[:, :col_width], n_ctx, me)
    got_dy = to_experts(place(cotangent))
    grads_in = gather_blocks(got_dy, n_ctx, me)

    group = w_gate.shape[2]
    gate_w = w_gate[0].reshape(n_ctx, col_width, group)
    up_w = w_up[0].reshape(n_ctx, col_width, group)
    down_w = w_down[0]
    down_cols = [down_w[:, q * col_width : (q + 1) * col_width] for q in range(n_ctx)]

    pre_gate = jnp.einsum("nsd,ndf->sf", rows_in, gate_w, preferred_element_type=jnp.float32)
    pre_up = jnp.einsum("nsd,ndf->sf", rows_in, up_w, preferred_element_type=jnp.float32)
    sigma = jax.nn.sigmoid(pre_gate)
    activated = pre_gate * sigma
    hidden = (activated * pre_up).astype(jnp.bfloat16)
    partial_out = jnp.stack(
        [jnp.dot(hidden, cols, preferred_element_type=jnp.float32) for cols in down_cols]
    ).astype(jnp.bfloat16)
    gate_part = jnp.einsum(
        "nsd,nsd->s", partial_out.astype(jnp.float32), grads_in.astype(jnp.float32)
    )
    gate_cols = with_cols(jnp.zeros((slot_count, 0), jnp.bfloat16), gate_part, pad)
    out_parts = jnp.concatenate(
        [partial_out, jnp.broadcast_to(gate_cols[None], (n_ctx, slot_count, pad))], axis=2
    )
    out_sums = scatter_sum(out_parts.astype(jnp.float32), n_ctx, me)
    expert_out = out_sums[:, :col_width].astype(jnp.bfloat16)
    gate_sum = out_sums[:, col_width] + out_sums[:, col_width + 1]
    back_out = to_experts(with_cols(expert_out, gate_sum, pad))

    contract_last = (((1,), (1,)), ((), ()))
    down_t = sum(
        lax.dot_general(grads_in[q], down_cols[q], contract_last, preferred_element_type=jnp.float32)
        for q in range(n_ctx)
    )
    hidden_grad = gate_column * down_t
    grad_gate = (hidden_grad * pre_up * sigma * (1.0 + pre_gate * (1.0 - sigma))).astype(
        jnp.bfloat16
    )
    grad_up = (hidden_grad * activated).astype(jnp.bfloat16)
    back_terms = jnp.einsum(
        "sf,ndf->nsd", grad_gate, gate_w, preferred_element_type=jnp.float32
    ) + jnp.einsum("sf,ndf->nsd", grad_up, up_w, preferred_element_type=jnp.float32)
    back_terms = back_terms.astype(jnp.bfloat16).astype(jnp.float32)
    slot_grad = scatter_sum(back_terms, n_ctx, me).astype(jnp.bfloat16)
    back_grad = to_experts(slot_grad)

    w_gate_grad = jnp.einsum(
        "nsd,sf->ndf", rows_in, grad_gate, preferred_element_type=jnp.float32
    ).astype(jnp.bfloat16).reshape(1, n_ctx * col_width, group)
    w_up_grad = jnp.einsum(
        "nsd,sf->ndf", rows_in, grad_up, preferred_element_type=jnp.float32
    ).astype(jnp.bfloat16).reshape(1, n_ctx * col_width, group)

    layer_out = jnp.zeros((tok_rows, col_width), jnp.float32)
    input_grad = jnp.zeros((tok_rows, col_width), jnp.float32)
    gate_terms = []
    for r, chosen in enumerate(route_maps):
        pick = chosen.astype(jnp.bfloat16)
        rows_r = jnp.dot(pick, back_out, preferred_element_type=jnp.float32)
        layer_out = layer_out + route_gates[:, r][:, None] * rows_r[:, :col_width]
        input_grad = input_grad + jnp.dot(pick, back_grad, preferred_element_type=jnp.float32)
        gate_terms.append(rows_r[:, col_width] + rows_r[:, col_width + 1])
    gate_grad = jnp.stack(gate_terms, axis=1)
    return (
        layer_out.astype(jnp.bfloat16),
        input_grad.astype(jnp.bfloat16),
        gate_grad,
        w_gate_grad,
        w_up_grad,
    )


def solution(mesh):
    in_specs = (
        P("ep", "ctx"),
        P("ep", "ctx"),
        P("ep", None),
        P("ep", None),
        P("ep", None, "ctx"),
        P("ep", None, "ctx"),
        P("ep", "ctx", None),
    )
    out_specs = (
        P("ep", "ctx"),
        P("ep", "ctx"),
        P("ep", None),
        P("ep", None, "ctx"),
        P("ep", None, "ctx"),
    )
    return jax.shard_map(shards, mesh=mesh, in_specs=in_specs, out_specs=out_specs, check_vma=False)
```

```python
import jax
import jax.numpy as jnp
from jax import lax
from jax.experimental import pallas as pl
from jax.sharding import PartitionSpec as P


def route_onehot(expert_ids, experts, capacity):
    tok_rows, routes = expert_ids.shape
    flat_ids = expert_ids.reshape(-1)
    labels = jnp.arange(experts, dtype=jnp.int32)
    onehot = (flat_ids[:, None] == labels[None, :]).astype(jnp.bfloat16)
    pairs = jnp.arange(flat_ids.shape[0], dtype=jnp.int32)
    before = (pairs[:, None] > pairs[None, :]).astype(jnp.bfloat16)
    earlier = jnp.dot(before, onehot, preferred_element_type=jnp.float32)
    slot_rank = jnp.sum(earlier * onehot.astype(jnp.float32), axis=1).astype(jnp.int32)
    slot_ids = (flat_ids * capacity + slot_rank).reshape(tok_rows, routes)
    positions = jnp.arange(experts * capacity, dtype=jnp.int32)
    return [slot_ids[:, r][:, None] == positions[None, :] for r in range(routes)]


def split_f32(values):
    hi = values.astype(jnp.bfloat16)
    lo = (values - hi.astype(jnp.float32)).astype(jnp.bfloat16)
    return hi, lo


def join_f32(hi, lo):
    return hi.astype(jnp.float32) + lo.astype(jnp.float32)


def ctx_bits(n_ctx):
    bits = n_ctx.bit_length() - 1
    assert 1 << bits == n_ctx
    return bits


def xor_pairs(n_ctx, bit):
    return [(i, i ^ (1 << bit)) for i in range(n_ctx)]


def gather_blocks(block, n_ctx, me):
    held = block[None]
    for bit in reversed(range(ctx_bits(n_ctx))):
        other = lax.ppermute(held, "ctx", xor_pairs(n_ctx, bit))
        mine_first = ((me >> bit) & 1) == 0
        pair = jnp.where(
            mine_first, jnp.stack([held, other], axis=1), jnp.stack([other, held], axis=1)
        )
        held = pair.reshape((-1,) + block.shape)
    return held


def scatter_sum(blocks, n_ctx, me):
    acc = blocks
    for bit in range(ctx_bits(n_ctx)):
        halves = acc.reshape((-1, 2) + acc.shape[1:])
        keep_first = ((me >> bit) & 1) == 0
        keep = jnp.where(keep_first, halves[:, 0], halves[:, 1])
        send = jnp.where(keep_first, halves[:, 1], halves[:, 0]).astype(jnp.bfloat16)
        got = lax.ppermute(send, "ctx", xor_pairs(n_ctx, bit))
        acc = keep + got.astype(jnp.float32)
    return acc[0]


def all_sum(values, n_ctx):
    for bit in range(ctx_bits(n_ctx)):
        values = values + lax.ppermute(values, "ctx", xor_pairs(n_ctx, bit))
    return values


def with_cols(rows, values, pad):
    hi, lo = split_f32(values)
    zeros = jnp.zeros((rows.shape[0], pad - 2), jnp.bfloat16)
    return jnp.concatenate([rows, hi[:, None], lo[:, None], zeros], axis=1)


def pre_kernel(x_ref, wg_ref, wu_ref, pg_ref, pu_ref):
    @pl.when(pl.program_id(0) == 0)
    def _():
        pg_ref[...] = jnp.zeros_like(pg_ref)
        pu_ref[...] = jnp.zeros_like(pu_ref)

    x = x_ref[0]
    pg_ref[...] += jnp.dot(x, wg_ref[...], preferred_element_type=jnp.float32)
    pu_ref[...] += jnp.dot(x, wu_ref[...], preferred_element_type=jnp.float32)


def pre_projections(rows_in, gate_w, up_w):
    n, slots, width = rows_in.shape
    group = gate_w.shape[1]
    out = jax.ShapeDtypeStruct((slots, group), jnp.float32)
    return pl.pallas_call(
        pre_kernel,
        grid=(n,),
        in_specs=[
            pl.BlockSpec((1, slots, width), lambda q: (q, 0, 0)),
            pl.BlockSpec((width, group), lambda q: (q, 0)),
            pl.BlockSpec((width, group), lambda q: (q, 0)),
        ],
        out_specs=[
            pl.BlockSpec((slots, group), lambda q: (0, 0)),
            pl.BlockSpec((slots, group), lambda q: (0, 0)),
        ],
        out_shape=[out, out],
    )(rows_in, gate_w, up_w)


def shards(tokens, cotangent, expert_ids, route_gates, w_gate, w_up, w_down):
    tok_rows, routes = expert_ids.shape
    experts = lax.axis_size("ep")
    n_ctx = lax.axis_size("ctx")
    me = lax.axis_index("ctx")
    capacity = 3 * tok_rows * routes // (2 * experts)
    slot_count = experts * capacity
    col_width = tokens.shape[1]
    pad = 128
    route_maps = route_onehot(expert_ids, experts, capacity)

    def place(values):
        placed = jnp.zeros((slot_count, values.shape[1]), jnp.float32)
        for chosen in route_maps:
            placed = placed + jnp.einsum(
                "ts,tc->sc", chosen.astype(jnp.bfloat16), values, preferred_element_type=jnp.float32
            )
        return placed.astype(jnp.bfloat16)

    def to_experts(rows):
        sent = rows.reshape(experts, capacity, rows.shape[1])
        got = lax.all_to_all(sent, "ep", split_axis=0, concat_axis=0, tiled=True)
        return got.reshape(slot_count, rows.shape[1])

    slot_gates = jnp.zeros((slot_count,), jnp.float32)
    for r, chosen in enumerate(route_maps):
        slot_gates = slot_gates + jnp.sum(jnp.where(chosen, route_gates[:, r][:, None], 0.0), axis=0)
    got_x = to_experts(with_cols(place(tokens), slot_gates, pad))
    gate_column = join_f32(got_x[:, col_width], got_x[:, col_width + 1])[:, None]
    rows_in = gather_blocks(got_x[:, :col_width], n_ctx, me)
    got_dy = to_experts(place(cotangent))
    grads_in = gather_blocks(got_dy, n_ctx, me)

    group = w_gate.shape[2]
    gate_w = w_gate[0].reshape(n_ctx, col_width, group)
    up_w = w_up[0].reshape(n_ctx, col_width, group)
    down_w = w_down[0]
    down_cols = [down_w[:, q * col_width : (q + 1) * col_width] for q in range(n_ctx)]

    pre_gate, pre_up = pre_projections(rows_in, w_gate[0], w_up[0])
    sigma = jax.nn.sigmoid(pre_gate)
    activated = pre_gate * sigma
    hidden = (activated * pre_up).astype(jnp.bfloat16)
    partial_out = jnp.stack(
        [jnp.dot(hidden, cols, preferred_element_type=jnp.float32) for cols in down_cols]
    ).astype(jnp.bfloat16)
    gate_part = jnp.einsum(
        "nsd,nsd->s", partial_out.astype(jnp.float32), grads_in.astype(jnp.float32)
    )
    expert_out = scatter_sum(partial_out.astype(jnp.float32), n_ctx, me).astype(jnp.bfloat16)
    gate_sum = all_sum(gate_part, n_ctx)
    back_out = to_experts(with_cols(expert_out, gate_sum, pad))

    contract_last = (((1,), (1,)), ((), ()))
    down_t = sum(
        lax.dot_general(grads_in[q], down_cols[q], contract_last, preferred_element_type=jnp.float32)
        for q in range(n_ctx)
    )
    hidden_grad = gate_column * down_t
    grad_gate = (hidden_grad * pre_up * sigma * (1.0 + pre_gate * (1.0 - sigma))).astype(
        jnp.bfloat16
    )
    grad_up = (hidden_grad * activated).astype(jnp.bfloat16)
    back_terms = jnp.einsum(
        "sf,ndf->nsd", grad_gate, gate_w, preferred_element_type=jnp.float32
    ) + jnp.einsum("sf,ndf->nsd", grad_up, up_w, preferred_element_type=jnp.float32)
    back_terms = back_terms.astype(jnp.bfloat16).astype(jnp.float32)
    slot_grad = scatter_sum(back_terms, n_ctx, me).astype(jnp.bfloat16)
    back_grad = to_experts(slot_grad)

    w_gate_grad = jnp.einsum(
        "nsd,sf->ndf", rows_in, grad_gate, preferred_element_type=jnp.float32
    ).astype(jnp.bfloat16).reshape(1, n_ctx * col_width, group)
    w_up_grad = jnp.einsum(
        "nsd,sf->ndf", rows_in, grad_up, preferred_element_type=jnp.float32
    ).astype(jnp.bfloat16).reshape(1, n_ctx * col_width, group)

    layer_out = jnp.zeros((tok_rows, col_width), jnp.float32)
    input_grad = jnp.zeros((tok_rows, col_width), jnp.float32)
    gate_terms = []
    for r, chosen in enumerate(route_maps):
        pick = chosen.astype(jnp.bfloat16)
        rows_r = jnp.dot(pick, back_out, preferred_element_type=jnp.float32)
        layer_out = layer_out + route_gates[:, r][:, None] * rows_r[:, :col_width]
        input_grad = input_grad + jnp.dot(pick, back_grad, preferred_element_type=jnp.float32)
        gate_terms.append(rows_r[:, col_width] + rows_r[:, col_width + 1])
    gate_grad = jnp.stack(gate_terms, axis=1)
    return (
        layer_out.astype(jnp.bfloat16),
        input_grad.astype(jnp.bfloat16),
        gate_grad,
        w_gate_grad,
        w_up_grad,
    )


def solution(mesh):
    in_specs = (
        P("ep", "ctx"),
        P("ep", "ctx"),
        P("ep", None),
        P("ep", None),
        P("ep", None, "ctx"),
        P("ep", None, "ctx"),
        P("ep", "ctx", None),
    )
    out_specs = (
        P("ep", "ctx"),
        P("ep", "ctx"),
        P("ep", None),
        P("ep", None, "ctx"),
        P("ep", None, "ctx"),
    )
    return jax.shard_map(shards, mesh=mesh, in_specs=in_specs, out_specs=out_specs, check_vma=False)
```

```python
import jax
import jax.numpy as jnp
from jax import lax
from jax.sharding import PartitionSpec as P


def route_onehot(expert_ids, experts, capacity):
    tok_rows, routes = expert_ids.shape
    flat_ids = expert_ids.reshape(-1)
    labels = jnp.arange(experts, dtype=jnp.int32)
    onehot = (flat_ids[:, None] == labels[None, :]).astype(jnp.bfloat16)
    pairs = jnp.arange(flat_ids.shape[0], dtype=jnp.int32)
    before = (pairs[:, None] > pairs[None, :]).astype(jnp.bfloat16)
    earlier = jnp.dot(before, onehot, preferred_element_type=jnp.float32)
    slot_rank = jnp.sum(earlier * onehot.astype(jnp.float32), axis=1).astype(jnp.int32)
    slot_ids = (flat_ids * capacity + slot_rank).reshape(tok_rows, routes)
    positions = jnp.arange(experts * capacity, dtype=jnp.int32)
    return [slot_ids[:, r][:, None] == positions[None, :] for r in range(routes)]


def split_f32(values):
    hi = values.astype(jnp.bfloat16)
    lo = (values - hi.astype(jnp.float32)).astype(jnp.bfloat16)
    return hi, lo


def join_f32(hi, lo):
    return hi.astype(jnp.float32) + lo.astype(jnp.float32)


def ctx_bits(n_ctx):
    bits = n_ctx.bit_length() - 1
    assert 1 << bits == n_ctx
    return bits


def xor_pairs(n_ctx, bit):
    return [(i, i ^ (1 << bit)) for i in range(n_ctx)]


def gather_blocks(block, n_ctx, me):
    held = block[None]
    for bit in reversed(range(ctx_bits(n_ctx))):
        other = lax.ppermute(held, "ctx", xor_pairs(n_ctx, bit))
        mine_first = ((me >> bit) & 1) == 0
        pair = jnp.where(
            mine_first, jnp.stack([held, other], axis=1), jnp.stack([other, held], axis=1)
        )
        held = pair.reshape((-1,) + block.shape)
    return held


def after(values, needed):
    zero = needed[(0,) * needed.ndim].astype(jnp.float32) * 0.0
    return values + zero.astype(values.dtype)


def scatter_sum(blocks, n_ctx, me):
    acc = blocks
    for bit in range(ctx_bits(n_ctx)):
        halves = acc.reshape((-1, 2) + acc.shape[1:])
        keep_first = ((me >> bit) & 1) == 0
        keep = jnp.where(keep_first, halves[:, 0], halves[:, 1])
        send = jnp.where(keep_first, halves[:, 1], halves[:, 0]).astype(jnp.bfloat16)
        got = lax.ppermute(send, "ctx", xor_pairs(n_ctx, bit))
        acc = keep + got.astype(jnp.float32)
    return acc[0]


def all_sum(values, n_ctx):
    for bit in range(ctx_bits(n_ctx)):
        values = values + lax.ppermute(values, "ctx", xor_pairs(n_ctx, bit))
    return values


def with_cols(rows, values, pad):
    hi, lo = split_f32(values)
    zeros = jnp.zeros((rows.shape[0], pad - 2), jnp.bfloat16)
    return jnp.concatenate([rows, hi[:, None], lo[:, None], zeros], axis=1)


def shards(tokens, cotangent, expert_ids, route_gates, w_gate, w_up, w_down):
    tok_rows, routes = expert_ids.shape
    experts = lax.axis_size("ep")
    n_ctx = lax.axis_size("ctx")
    me = lax.axis_index("ctx")
    capacity = 3 * tok_rows * routes // (2 * experts)
    slot_count = experts * capacity
    col_width = tokens.shape[1]
    pad = 128
    route_maps = route_onehot(expert_ids, experts, capacity)

    def place(values):
        placed = jnp.zeros((slot_count, values.shape[1]), jnp.float32)
        for chosen in route_maps:
            placed = placed + jnp.einsum(
                "ts,tc->sc", chosen.astype(jnp.bfloat16), values, preferred_element_type=jnp.float32
            )
        return placed.astype(jnp.bfloat16)

    def to_experts(rows):
        sent = rows.reshape(experts, capacity, rows.shape[1])
        got = lax.all_to_all(sent, "ep", split_axis=0, concat_axis=0, tiled=True)
        return got.reshape(slot_count, rows.shape[1])

    slot_gates = jnp.zeros((slot_count,), jnp.float32)
    for r, chosen in enumerate(route_maps):
        slot_gates = slot_gates + jnp.sum(jnp.where(chosen, route_gates[:, r][:, None], 0.0), axis=0)
    got_x = to_experts(with_cols(place(tokens), slot_gates, pad))
    gate_column = join_f32(got_x[:, col_width], got_x[:, col_width + 1])[:, None]
    rows_in = gather_blocks(got_x[:, :col_width], n_ctx, me)
    got_dy = to_experts(after(place(cotangent), got_x))
    grads_in = gather_blocks(got_dy, n_ctx, me)

    group = w_gate.shape[2]
    gate_w = w_gate[0].reshape(n_ctx, col_width, group)
    up_w = w_up[0].reshape(n_ctx, col_width, group)
    down_w = w_down[0]
    down_cols = [down_w[:, q * col_width : (q + 1) * col_width] for q in range(n_ctx)]

    pre_gate = jnp.einsum("nsd,ndf->sf", rows_in, gate_w, preferred_element_type=jnp.float32)
    pre_up = jnp.einsum("nsd,ndf->sf", rows_in, up_w, preferred_element_type=jnp.float32)
    sigma = jax.nn.sigmoid(pre_gate)
    activated = pre_gate * sigma
    hidden = (activated * pre_up).astype(jnp.bfloat16)
    partial_out = jnp.stack(
        [jnp.dot(hidden, cols, preferred_element_type=jnp.float32) for cols in down_cols]
    ).astype(jnp.bfloat16)
    gate_part = jnp.einsum(
        "nsd,nsd->s", partial_out.astype(jnp.float32), grads_in.astype(jnp.float32)
    )
    expert_out = scatter_sum(partial_out.astype(jnp.float32), n_ctx, me).astype(jnp.bfloat16)
    gate_sum = all_sum(gate_part, n_ctx)
    back_out = to_experts(with_cols(expert_out, gate_sum, pad))

    contract_last = (((1,), (1,)), ((), ()))
    down_t = sum(
        lax.dot_general(grads_in[q], down_cols[q], contract_last, preferred_element_type=jnp.float32)
        for q in range(n_ctx)
    )
    hidden_grad = gate_column * down_t
    grad_gate = (hidden_grad * pre_up * sigma * (1.0 + pre_gate * (1.0 - sigma))).astype(
        jnp.bfloat16
    )
    grad_up = (hidden_grad * activated).astype(jnp.bfloat16)
    back_terms = jnp.einsum(
        "sf,ndf->nsd", grad_gate, gate_w, preferred_element_type=jnp.float32
    ) + jnp.einsum("sf,ndf->nsd", grad_up, up_w, preferred_element_type=jnp.float32)
    back_terms = back_terms.astype(jnp.bfloat16).astype(jnp.float32)
    slot_grad = scatter_sum(back_terms, n_ctx, me).astype(jnp.bfloat16)
    back_grad = to_experts(slot_grad)

    w_gate_grad = jnp.einsum(
        "nsd,sf->ndf", rows_in, grad_gate, preferred_element_type=jnp.float32
    ).astype(jnp.bfloat16).reshape(1, n_ctx * col_width, group)
    w_up_grad = jnp.einsum(
        "nsd,sf->ndf", rows_in, grad_up, preferred_element_type=jnp.float32
    ).astype(jnp.bfloat16).reshape(1, n_ctx * col_width, group)

    layer_out = jnp.zeros((tok_rows, col_width), jnp.float32)
    input_grad = jnp.zeros((tok_rows, col_width), jnp.float32)
    gate_terms = []
    for r, chosen in enumerate(route_maps):
        pick = chosen.astype(jnp.bfloat16)
        rows_r = jnp.dot(pick, back_out, preferred_element_type=jnp.float32)
        layer_out = layer_out + route_gates[:, r][:, None] * rows_r[:, :col_width]
        input_grad = input_grad + jnp.dot(pick, back_grad, preferred_element_type=jnp.float32)
        gate_terms.append(rows_r[:, col_width] + rows_r[:, col_width + 1])
    gate_grad = jnp.stack(gate_terms, axis=1)
    return (
        layer_out.astype(jnp.bfloat16),
        input_grad.astype(jnp.bfloat16),
        gate_grad,
        w_gate_grad,
        w_up_grad,
    )


def solution(mesh):
    in_specs = (
        P("ep", "ctx"),
        P("ep", "ctx"),
        P("ep", None),
        P("ep", None),
        P("ep", None, "ctx"),
        P("ep", None, "ctx"),
        P("ep", "ctx", None),
    )
    out_specs = (
        P("ep", "ctx"),
        P("ep", "ctx"),
        P("ep", None),
        P("ep", None, "ctx"),
        P("ep", None, "ctx"),
    )
    return jax.shard_map(shards, mesh=mesh, in_specs=in_specs, out_specs=out_specs, check_vma=False)
```

```python
import jax
import jax.numpy as jnp
from jax import lax
from jax.sharding import PartitionSpec as P


def route_onehot(expert_ids, experts, capacity):
    tok_rows, routes = expert_ids.shape
    flat_ids = expert_ids.reshape(-1)
    labels = jnp.arange(experts, dtype=jnp.int32)
    onehot = (flat_ids[:, None] == labels[None, :]).astype(jnp.bfloat16)
    pairs = jnp.arange(flat_ids.shape[0], dtype=jnp.int32)
    before = (pairs[:, None] > pairs[None, :]).astype(jnp.bfloat16)
    earlier = jnp.dot(before, onehot, preferred_element_type=jnp.float32)
    slot_rank = jnp.sum(earlier * onehot.astype(jnp.float32), axis=1).astype(jnp.int32)
    slot_ids = (flat_ids * capacity + slot_rank).reshape(tok_rows, routes)
    positions = jnp.arange(experts * capacity, dtype=jnp.int32)
    return [slot_ids[:, r][:, None] == positions[None, :] for r in range(routes)]


def split_f32(values):
    hi = values.astype(jnp.bfloat16)
    lo = (values - hi.astype(jnp.float32)).astype(jnp.bfloat16)
    return hi, lo


def join_f32(hi, lo):
    return hi.astype(jnp.float32) + lo.astype(jnp.float32)


def ctx_bits(n_ctx):
    bits = n_ctx.bit_length() - 1
    assert 1 << bits == n_ctx
    return bits


def xor_pairs(n_ctx, bit):
    return [(i, i ^ (1 << bit)) for i in range(n_ctx)]


def gather_blocks(block, n_ctx, me):
    held = block[None]
    for bit in reversed(range(ctx_bits(n_ctx))):
        other = lax.ppermute(held, "ctx", xor_pairs(n_ctx, bit))
        mine_first = ((me >> bit) & 1) == 0
        pair = jnp.where(
            mine_first, jnp.stack([held, other], axis=1), jnp.stack([other, held], axis=1)
        )
        held = pair.reshape((-1,) + block.shape)
    return held


def scatter_sum(blocks, n_ctx, me):
    acc = blocks
    for bit in range(ctx_bits(n_ctx)):
        halves = acc.reshape((-1, 2) + acc.shape[1:])
        keep_first = ((me >> bit) & 1) == 0
        keep = jnp.where(keep_first, halves[:, 0], halves[:, 1])
        send = jnp.where(keep_first, halves[:, 1], halves[:, 0]).astype(jnp.bfloat16)
        got = lax.ppermute(send, "ctx", xor_pairs(n_ctx, bit))
        acc = keep + got.astype(jnp.float32)
    return acc[0]


def all_sum(values, n_ctx):
    for bit in range(ctx_bits(n_ctx)):
        values = values + lax.ppermute(values, "ctx", xor_pairs(n_ctx, bit))
    return values


def with_cols(rows, values, pad):
    hi, lo = split_f32(values)
    zeros = jnp.zeros((rows.shape[0], pad - 2), jnp.bfloat16)
    return jnp.concatenate([rows, hi[:, None], lo[:, None], zeros], axis=1)


def shards(tokens, cotangent, expert_ids, route_gates, w_gate, w_up, w_down):
    tok_rows, routes = expert_ids.shape
    experts = lax.axis_size("ep")
    n_ctx = lax.axis_size("ctx")
    me = lax.axis_index("ctx")
    capacity = 3 * tok_rows * routes // (2 * experts)
    slot_count = experts * capacity
    col_width = tokens.shape[1]
    pad = 128
    route_maps = route_onehot(expert_ids, experts, capacity)

    def place(values):
        placed = jnp.zeros((slot_count, values.shape[1]), jnp.float32)
        for chosen in route_maps:
            placed = placed + jnp.einsum(
                "ts,tc->sc", chosen.astype(jnp.bfloat16), values, preferred_element_type=jnp.float32
            )
        return placed.astype(jnp.bfloat16)

    def to_experts(rows):
        sent = rows.reshape(experts, capacity, rows.shape[1])
        got = lax.all_to_all(sent, "ep", split_axis=0, concat_axis=0, tiled=True)
        return got.reshape(slot_count, rows.shape[1])

    slot_gates = jnp.zeros((slot_count,), jnp.float32)
    for r, chosen in enumerate(route_maps):
        slot_gates = slot_gates + jnp.sum(jnp.where(chosen, route_gates[:, r][:, None], 0.0), axis=0)
    got_x = to_experts(place(tokens))
    rows_in = gather_blocks(got_x, n_ctx, me)
    got_dy = to_experts(with_cols(place(cotangent), slot_gates, pad))
    gate_column = join_f32(got_dy[:, col_width], got_dy[:, col_width + 1])[:, None]
    grads_in = gather_blocks(got_dy[:, :col_width], n_ctx, me)

    group = w_gate.shape[2]
    gate_w = w_gate[0].reshape(n_ctx, col_width, group)
    up_w = w_up[0].reshape(n_ctx, col_width, group)
    down_w = w_down[0]
    down_cols = [down_w[:, q * col_width : (q + 1) * col_width] for q in range(n_ctx)]

    pre_gate = jnp.einsum("nsd,ndf->sf", rows_in, gate_w, preferred_element_type=jnp.float32)
    pre_up = jnp.einsum("nsd,ndf->sf", rows_in, up_w, preferred_element_type=jnp.float32)
    sigma = jax.nn.sigmoid(pre_gate)
    activated = pre_gate * sigma
    hidden = (activated * pre_up).astype(jnp.bfloat16)
    partial_out = jnp.stack(
        [jnp.dot(hidden, cols, preferred_element_type=jnp.float32) for cols in down_cols]
    ).astype(jnp.bfloat16)
    gate_part = jnp.einsum(
        "nsd,nsd->s", partial_out.astype(jnp.float32), grads_in.astype(jnp.float32)
    )
    expert_out = scatter_sum(partial_out.astype(jnp.float32), n_ctx, me).astype(jnp.bfloat16)
    gate_sum = all_sum(gate_part, n_ctx)
    back_out = to_experts(with_cols(expert_out, gate_sum, pad))

    contract_last = (((1,), (1,)), ((), ()))
    down_t = sum(
        lax.dot_general(grads_in[q], down_cols[q], contract_last, preferred_element_type=jnp.float32)
        for q in range(n_ctx)
    )
    hidden_grad = gate_column * down_t
    grad_gate = (hidden_grad * pre_up * sigma * (1.0 + pre_gate * (1.0 - sigma))).astype(
        jnp.bfloat16
    )
    grad_up = (hidden_grad * activated).astype(jnp.bfloat16)
    back_terms = jnp.einsum(
        "sf,ndf->nsd", grad_gate, gate_w, preferred_element_type=jnp.float32
    ) + jnp.einsum("sf,ndf->nsd", grad_up, up_w, preferred_element_type=jnp.float32)
    back_terms = back_terms.astype(jnp.bfloat16).astype(jnp.float32)
    slot_grad = scatter_sum(back_terms, n_ctx, me).astype(jnp.bfloat16)
    back_grad = to_experts(slot_grad)

    w_gate_grad = jnp.einsum(
        "nsd,sf->ndf", rows_in, grad_gate, preferred_element_type=jnp.float32
    ).astype(jnp.bfloat16).reshape(1, n_ctx * col_width, group)
    w_up_grad = jnp.einsum(
        "nsd,sf->ndf", rows_in, grad_up, preferred_element_type=jnp.float32
    ).astype(jnp.bfloat16).reshape(1, n_ctx * col_width, group)

    layer_out = jnp.zeros((tok_rows, col_width), jnp.float32)
    input_grad = jnp.zeros((tok_rows, col_width), jnp.float32)
    gate_terms = []
    for r, chosen in enumerate(route_maps):
        pick = chosen.astype(jnp.bfloat16)
        rows_r = jnp.dot(pick, back_out, preferred_element_type=jnp.float32)
        layer_out = layer_out + route_gates[:, r][:, None] * rows_r[:, :col_width]
        input_grad = input_grad + jnp.dot(pick, back_grad, preferred_element_type=jnp.float32)
        gate_terms.append(rows_r[:, col_width] + rows_r[:, col_width + 1])
    gate_grad = jnp.stack(gate_terms, axis=1)
    return (
        layer_out.astype(jnp.bfloat16),
        input_grad.astype(jnp.bfloat16),
        gate_grad,
        w_gate_grad,
        w_up_grad,
    )


def solution(mesh):
    in_specs = (
        P("ep", "ctx"),
        P("ep", "ctx"),
        P("ep", None),
        P("ep", None),
        P("ep", None, "ctx"),
        P("ep", None, "ctx"),
        P("ep", "ctx", None),
    )
    out_specs = (
        P("ep", "ctx"),
        P("ep", "ctx"),
        P("ep", None),
        P("ep", None, "ctx"),
        P("ep", None, "ctx"),
    )
    return jax.shard_map(shards, mesh=mesh, in_specs=in_specs, out_specs=out_specs, check_vma=False)
```

```python
import jax
import jax.numpy as jnp
from jax import lax
from jax.sharding import PartitionSpec as P


def route_onehot(expert_ids, experts, capacity):
    tok_rows, routes = expert_ids.shape
    flat_ids = expert_ids.reshape(-1)
    labels = jnp.arange(experts, dtype=jnp.int32)
    onehot = (flat_ids[:, None] == labels[None, :]).astype(jnp.bfloat16)
    pairs = jnp.arange(flat_ids.shape[0], dtype=jnp.int32)
    before = (pairs[:, None] > pairs[None, :]).astype(jnp.bfloat16)
    earlier = jnp.dot(before, onehot, preferred_element_type=jnp.float32)
    slot_rank = jnp.sum(earlier * onehot.astype(jnp.float32), axis=1).astype(jnp.int32)
    slot_ids = (flat_ids * capacity + slot_rank).reshape(tok_rows, routes)
    positions = jnp.arange(experts * capacity, dtype=jnp.int32)
    return [slot_ids[:, r][:, None] == positions[None, :] for r in range(routes)]


def split_f32(values):
    hi = values.astype(jnp.bfloat16)
    lo = (values - hi.astype(jnp.float32)).astype(jnp.bfloat16)
    return hi, lo


def join_f32(hi, lo):
    return hi.astype(jnp.float32) + lo.astype(jnp.float32)


def ctx_bits(n_ctx):
    bits = n_ctx.bit_length() - 1
    assert 1 << bits == n_ctx
    return bits


def xor_pairs(n_ctx, bit):
    return [(i, i ^ (1 << bit)) for i in range(n_ctx)]


def gather_blocks(block, n_ctx, me):
    held = block[None]
    for bit in reversed(range(ctx_bits(n_ctx))):
        other = lax.ppermute(held, "ctx", xor_pairs(n_ctx, bit))
        mine_first = ((me >> bit) & 1) == 0
        pair = jnp.where(
            mine_first, jnp.stack([held, other], axis=1), jnp.stack([other, held], axis=1)
        )
        held = pair.reshape((-1,) + block.shape)
    return held


def scatter_sum(blocks, n_ctx, me):
    acc = blocks
    for bit in range(ctx_bits(n_ctx)):
        halves = acc.reshape((-1, 2) + acc.shape[1:])
        keep_first = ((me >> bit) & 1) == 0
        keep = jnp.where(keep_first, halves[:, 0], halves[:, 1])
        send = jnp.where(keep_first, halves[:, 1], halves[:, 0]).astype(jnp.bfloat16)
        got = lax.ppermute(send, "ctx", xor_pairs(n_ctx, bit))
        acc = keep + got.astype(jnp.float32)
    return acc[0]


def pair_sum(first, second, n_ctx, me):
    width = first.shape[2]
    halves = jnp.concatenate([first, second], axis=2).reshape((-1, 2) + first.shape[1:2] + (2 * width,))
    keep_first = (me & 1) == 0
    keep = jnp.where(keep_first, halves[:, 0], halves[:, 1])
    send = jnp.where(keep_first, halves[:, 1], halves[:, 0]).astype(jnp.bfloat16)
    acc = keep + lax.ppermute(send, "ctx", xor_pairs(n_ctx, 0)).astype(jnp.float32)
    return [rest_sum(acc[:, :, :width], n_ctx, me), rest_sum(acc[:, :, width:], n_ctx, me)]


def rest_sum(acc, n_ctx, me):
    for bit in range(1, ctx_bits(n_ctx)):
        halves = acc.reshape((-1, 2) + acc.shape[1:])
        keep_first = ((me >> bit) & 1) == 0
        keep = jnp.where(keep_first, halves[:, 0], halves[:, 1])
        send = jnp.where(keep_first, halves[:, 1], halves[:, 0]).astype(jnp.bfloat16)
        got = lax.ppermute(send, "ctx", xor_pairs(n_ctx, bit))
        acc = keep + got.astype(jnp.float32)
    return acc[0]


def all_sum(values, n_ctx):
    for bit in range(ctx_bits(n_ctx)):
        values = values + lax.ppermute(values, "ctx", xor_pairs(n_ctx, bit))
    return values


def with_cols(rows, values, pad):
    hi, lo = split_f32(values)
    zeros = jnp.zeros((rows.shape[0], pad - 2), jnp.bfloat16)
    return jnp.concatenate([rows, hi[:, None], lo[:, None], zeros], axis=1)


def shards(tokens, cotangent, expert_ids, route_gates, w_gate, w_up, w_down):
    tok_rows, routes = expert_ids.shape
    experts = lax.axis_size("ep")
    n_ctx = lax.axis_size("ctx")
    me = lax.axis_index("ctx")
    capacity = 3 * tok_rows * routes // (2 * experts)
    slot_count = experts * capacity
    col_width = tokens.shape[1]
    pad = 128
    route_maps = route_onehot(expert_ids, experts, capacity)

    def place(values):
        placed = jnp.zeros((slot_count, values.shape[1]), jnp.float32)
        for chosen in route_maps:
            placed = placed + jnp.einsum(
                "ts,tc->sc", chosen.astype(jnp.bfloat16), values, preferred_element_type=jnp.float32
            )
        return placed.astype(jnp.bfloat16)

    def to_experts(rows):
        sent = rows.reshape(experts, capacity, rows.shape[1])
        got = lax.all_to_all(sent, "ep", split_axis=0, concat_axis=0, tiled=True)
        return got.reshape(slot_count, rows.shape[1])

    slot_gates = jnp.zeros((slot_count,), jnp.float32)
    for r, chosen in enumerate(route_maps):
        slot_gates = slot_gates + jnp.sum(jnp.where(chosen, route_gates[:, r][:, None], 0.0), axis=0)
    got_x = to_experts(with_cols(place(tokens), slot_gates, pad))
    gate_column = join_f32(got_x[:, col_width], got_x[:, col_width + 1])[:, None]
    rows_in = gather_blocks(got_x[:, :col_width], n_ctx, me)
    got_dy = to_experts(place(cotangent))
    grads_in = gather_blocks(got_dy, n_ctx, me)

    group = w_gate.shape[2]
    gate_w = w_gate[0].reshape(n_ctx, col_width, group)
    up_w = w_up[0].reshape(n_ctx, col_width, group)
    down_w = w_down[0]
    down_cols = [down_w[:, q * col_width : (q + 1) * col_width] for q in range(n_ctx)]

    pre_gate = jnp.einsum("nsd,ndf->sf", rows_in, gate_w, preferred_element_type=jnp.float32)
    pre_up = jnp.einsum("nsd,ndf->sf", rows_in, up_w, preferred_element_type=jnp.float32)
    sigma = jax.nn.sigmoid(pre_gate)
    activated = pre_gate * sigma
    hidden = (activated * pre_up).astype(jnp.bfloat16)
    partial_out = jnp.stack(
        [jnp.dot(hidden, cols, preferred_element_type=jnp.float32) for cols in down_cols]
    ).astype(jnp.bfloat16)
    gate_part = jnp.einsum(
        "nsd,nsd->s", partial_out.astype(jnp.float32), grads_in.astype(jnp.float32)
    )
    gate_sum = all_sum(gate_part, n_ctx)

    contract_last = (((1,), (1,)), ((), ()))
    down_t = sum(
        lax.dot_general(grads_in[q], down_cols[q], contract_last, preferred_element_type=jnp.float32)
        for q in range(n_ctx)
    )
    hidden_grad = gate_column * down_t
    grad_gate = (hidden_grad * pre_up * sigma * (1.0 + pre_gate * (1.0 - sigma))).astype(
        jnp.bfloat16
    )
    grad_up = (hidden_grad * activated).astype(jnp.bfloat16)
    back_terms = jnp.einsum(
        "sf,ndf->nsd", grad_gate, gate_w, preferred_element_type=jnp.float32
    ) + jnp.einsum("sf,ndf->nsd", grad_up, up_w, preferred_element_type=jnp.float32)
    back_terms = back_terms.astype(jnp.bfloat16).astype(jnp.float32)
    out_sum, grad_sum = pair_sum(partial_out.astype(jnp.float32), back_terms, n_ctx, me)
    expert_out = out_sum.astype(jnp.bfloat16)
    slot_grad = grad_sum.astype(jnp.bfloat16)
    back_out = to_experts(with_cols(expert_out, gate_sum, pad))
    back_grad = to_experts(slot_grad)

    w_gate_grad = jnp.einsum(
        "nsd,sf->ndf", rows_in, grad_gate, preferred_element_type=jnp.float32
    ).astype(jnp.bfloat16).reshape(1, n_ctx * col_width, group)
    w_up_grad = jnp.einsum(
        "nsd,sf->ndf", rows_in, grad_up, preferred_element_type=jnp.float32
    ).astype(jnp.bfloat16).reshape(1, n_ctx * col_width, group)

    layer_out = jnp.zeros((tok_rows, col_width), jnp.float32)
    input_grad = jnp.zeros((tok_rows, col_width), jnp.float32)
    gate_terms = []
    for r, chosen in enumerate(route_maps):
        pick = chosen.astype(jnp.bfloat16)
        rows_r = jnp.dot(pick, back_out, preferred_element_type=jnp.float32)
        layer_out = layer_out + route_gates[:, r][:, None] * rows_r[:, :col_width]
        input_grad = input_grad + jnp.dot(pick, back_grad, preferred_element_type=jnp.float32)
        gate_terms.append(rows_r[:, col_width] + rows_r[:, col_width + 1])
    gate_grad = jnp.stack(gate_terms, axis=1)
    return (
        layer_out.astype(jnp.bfloat16),
        input_grad.astype(jnp.bfloat16),
        gate_grad,
        w_gate_grad,
        w_up_grad,
    )


def solution(mesh):
    in_specs = (
        P("ep", "ctx"),
        P("ep", "ctx"),
        P("ep", None),
        P("ep", None),
        P("ep", None, "ctx"),
        P("ep", None, "ctx"),
        P("ep", "ctx", None),
    )
    out_specs = (
        P("ep", "ctx"),
        P("ep", "ctx"),
        P("ep", None),
        P("ep", None, "ctx"),
        P("ep", None, "ctx"),
    )
    return jax.shard_map(shards, mesh=mesh, in_specs=in_specs, out_specs=out_specs, check_vma=False)
```

```python
import jax
import jax.numpy as jnp
from jax import lax
from jax.sharding import PartitionSpec as P


def route_onehot(expert_ids, experts, capacity):
    tok_rows, routes = expert_ids.shape
    flat_ids = expert_ids.reshape(-1)
    labels = jnp.arange(experts, dtype=jnp.int32)
    onehot = (flat_ids[:, None] == labels[None, :]).astype(jnp.bfloat16)
    pairs = jnp.arange(flat_ids.shape[0], dtype=jnp.int32)
    before = (pairs[:, None] > pairs[None, :]).astype(jnp.bfloat16)
    earlier = jnp.dot(before, onehot, preferred_element_type=jnp.float32)
    slot_rank = jnp.sum(earlier * onehot.astype(jnp.float32), axis=1).astype(jnp.int32)
    slot_ids = (flat_ids * capacity + slot_rank).reshape(tok_rows, routes)
    positions = jnp.arange(experts * capacity, dtype=jnp.int32)
    return [slot_ids[:, r][:, None] == positions[None, :] for r in range(routes)]


def split_f32(values):
    hi = values.astype(jnp.bfloat16)
    lo = (values - hi.astype(jnp.float32)).astype(jnp.bfloat16)
    return hi, lo


def join_f32(hi, lo):
    return hi.astype(jnp.float32) + lo.astype(jnp.float32)


def ctx_bits(n_ctx):
    bits = n_ctx.bit_length() - 1
    assert 1 << bits == n_ctx
    return bits


def xor_pairs(n_ctx, bit):
    return [(i, i ^ (1 << bit)) for i in range(n_ctx)]


def gather_blocks(block, n_ctx, me):
    held = block[None]
    masks = [0]
    for bit in reversed(range(ctx_bits(n_ctx))):
        other = lax.ppermute(held, "ctx", xor_pairs(n_ctx, bit))
        held = jnp.concatenate([held, other], axis=0)
        masks = masks + [m ^ (1 << bit) for m in masks]
    slot_of = [0] * n_ctx
    for j, m in enumerate(masks):
        slot_of[m] = j
    order = jnp.asarray(slot_of, jnp.int32)[jnp.arange(n_ctx, dtype=jnp.int32) ^ me]
    return jnp.take(held, order, axis=0)


def scatter_sum(blocks, n_ctx, me):
    acc = blocks
    for bit in range(ctx_bits(n_ctx)):
        halves = acc.reshape((-1, 2) + acc.shape[1:])
        keep_first = ((me >> bit) & 1) == 0
        keep = jnp.where(keep_first, halves[:, 0], halves[:, 1])
        send = jnp.where(keep_first, halves[:, 1], halves[:, 0]).astype(jnp.bfloat16)
        got = lax.ppermute(send, "ctx", xor_pairs(n_ctx, bit))
        acc = keep + got.astype(jnp.float32)
    return acc[0]


def all_sum(values, n_ctx):
    for bit in range(ctx_bits(n_ctx)):
        values = values + lax.ppermute(values, "ctx", xor_pairs(n_ctx, bit))
    return values


def with_cols(rows, values, pad):
    hi, lo = split_f32(values)
    zeros = jnp.zeros((rows.shape[0], pad - 2), jnp.bfloat16)
    return jnp.concatenate([rows, hi[:, None], lo[:, None], zeros], axis=1)


def shards(tokens, cotangent, expert_ids, route_gates, w_gate, w_up, w_down):
    tok_rows, routes = expert_ids.shape
    experts = lax.axis_size("ep")
    n_ctx = lax.axis_size("ctx")
    me = lax.axis_index("ctx")
    capacity = 3 * tok_rows * routes // (2 * experts)
    slot_count = experts * capacity
    col_width = tokens.shape[1]
    pad = 128
    route_maps = route_onehot(expert_ids, experts, capacity)

    def place(values):
        placed = jnp.zeros((slot_count, values.shape[1]), jnp.float32)
        for chosen in route_maps:
            placed = placed + jnp.einsum(
                "ts,tc->sc", chosen.astype(jnp.bfloat16), values, preferred_element_type=jnp.float32
            )
        return placed.astype(jnp.bfloat16)

    def to_experts(rows):
        sent = rows.reshape(experts, capacity, rows.shape[1])
        got = lax.all_to_all(sent, "ep", split_axis=0, concat_axis=0, tiled=True)
        return got.reshape(slot_count, rows.shape[1])

    slot_gates = jnp.zeros((slot_count,), jnp.float32)
    for r, chosen in enumerate(route_maps):
        slot_gates = slot_gates + jnp.sum(jnp.where(chosen, route_gates[:, r][:, None], 0.0), axis=0)
    got_x = to_experts(with_cols(place(tokens), slot_gates, pad))
    gate_column = join_f32(got_x[:, col_width], got_x[:, col_width + 1])[:, None]
    rows_in = gather_blocks(got_x[:, :col_width], n_ctx, me)
    got_dy = to_experts(place(cotangent))
    grads_in = gather_blocks(got_dy, n_ctx, me)

    group = w_gate.shape[2]
    gate_w = w_gate[0].reshape(n_ctx, col_width, group)
    up_w = w_up[0].reshape(n_ctx, col_width, group)
    down_w = w_down[0]
    down_cols = [down_w[:, q * col_width : (q + 1) * col_width] for q in range(n_ctx)]

    pre_gate = jnp.einsum("nsd,ndf->sf", rows_in, gate_w, preferred_element_type=jnp.float32)
    pre_up = jnp.einsum("nsd,ndf->sf", rows_in, up_w, preferred_element_type=jnp.float32)
    sigma = jax.nn.sigmoid(pre_gate)
    activated = pre_gate * sigma
    hidden = (activated * pre_up).astype(jnp.bfloat16)
    partial_out = jnp.stack(
        [jnp.dot(hidden, cols, preferred_element_type=jnp.float32) for cols in down_cols]
    ).astype(jnp.bfloat16)
    gate_part = jnp.einsum(
        "nsd,nsd->s", partial_out.astype(jnp.float32), grads_in.astype(jnp.float32)
    )
    expert_out = scatter_sum(partial_out.astype(jnp.float32), n_ctx, me).astype(jnp.bfloat16)
    gate_sum = all_sum(gate_part, n_ctx)
    back_out = to_experts(with_cols(expert_out, gate_sum, pad))

    contract_last = (((1,), (1,)), ((), ()))
    down_t = sum(
        lax.dot_general(grads_in[q], down_cols[q], contract_last, preferred_element_type=jnp.float32)
        for q in range(n_ctx)
    )
    hidden_grad = gate_column * down_t
    grad_gate = (hidden_grad * pre_up * sigma * (1.0 + pre_gate * (1.0 - sigma))).astype(
        jnp.bfloat16
    )
    grad_up = (hidden_grad * activated).astype(jnp.bfloat16)
    back_terms = jnp.einsum(
        "sf,ndf->nsd", grad_gate, gate_w, preferred_element_type=jnp.float32
    ) + jnp.einsum("sf,ndf->nsd", grad_up, up_w, preferred_element_type=jnp.float32)
    back_terms = back_terms.astype(jnp.bfloat16).astype(jnp.float32)
    slot_grad = scatter_sum(back_terms, n_ctx, me).astype(jnp.bfloat16)
    back_grad = to_experts(slot_grad)

    w_gate_grad = jnp.einsum(
        "nsd,sf->ndf", rows_in, grad_gate, preferred_element_type=jnp.float32
    ).astype(jnp.bfloat16).reshape(1, n_ctx * col_width, group)
    w_up_grad = jnp.einsum(
        "nsd,sf->ndf", rows_in, grad_up, preferred_element_type=jnp.float32
    ).astype(jnp.bfloat16).reshape(1, n_ctx * col_width, group)

    layer_out = jnp.zeros((tok_rows, col_width), jnp.float32)
    input_grad = jnp.zeros((tok_rows, col_width), jnp.float32)
    gate_terms = []
    for r, chosen in enumerate(route_maps):
        pick = chosen.astype(jnp.bfloat16)
        rows_r = jnp.dot(pick, back_out, preferred_element_type=jnp.float32)
        layer_out = layer_out + route_gates[:, r][:, None] * rows_r[:, :col_width]
        input_grad = input_grad + jnp.dot(pick, back_grad, preferred_element_type=jnp.float32)
        gate_terms.append(rows_r[:, col_width] + rows_r[:, col_width + 1])
    gate_grad = jnp.stack(gate_terms, axis=1)
    return (
        layer_out.astype(jnp.bfloat16),
        input_grad.astype(jnp.bfloat16),
        gate_grad,
        w_gate_grad,
        w_up_grad,
    )


def solution(mesh):
    in_specs = (
        P("ep", "ctx"),
        P("ep", "ctx"),
        P("ep", None),
        P("ep", None),
        P("ep", None, "ctx"),
        P("ep", None, "ctx"),
        P("ep", "ctx", None),
    )
    out_specs = (
        P("ep", "ctx"),
        P("ep", "ctx"),
        P("ep", None),
        P("ep", None, "ctx"),
        P("ep", None, "ctx"),
    )
    return jax.shard_map(shards, mesh=mesh, in_specs=in_specs, out_specs=out_specs, check_vma=False)
```

```python
import jax
import jax.numpy as jnp
from jax import lax
from jax.sharding import PartitionSpec as P


def route_onehot(expert_ids, experts, capacity):
    tok_rows, routes = expert_ids.shape
    flat_ids = expert_ids.reshape(-1)
    labels = jnp.arange(experts, dtype=jnp.int32)
    onehot = (flat_ids[:, None] == labels[None, :]).astype(jnp.bfloat16)
    pairs = jnp.arange(flat_ids.shape[0], dtype=jnp.int32)
    before = (pairs[:, None] > pairs[None, :]).astype(jnp.bfloat16)
    earlier = jnp.dot(before, onehot, preferred_element_type=jnp.float32)
    slot_rank = jnp.sum(earlier * onehot.astype(jnp.float32), axis=1).astype(jnp.int32)
    slot_ids = (flat_ids * capacity + slot_rank).reshape(tok_rows, routes)
    positions = jnp.arange(experts * capacity, dtype=jnp.int32)
    return [slot_ids[:, r][:, None] == positions[None, :] for r in range(routes)]


def split_f32(values):
    hi = values.astype(jnp.bfloat16)
    lo = (values - hi.astype(jnp.float32)).astype(jnp.bfloat16)
    return hi, lo


def join_f32(hi, lo):
    return hi.astype(jnp.float32) + lo.astype(jnp.float32)


def ctx_bits(n_ctx):
    bits = n_ctx.bit_length() - 1
    assert 1 << bits == n_ctx
    return bits


def xor_pairs(n_ctx, bit):
    return [(i, i ^ (1 << bit)) for i in range(n_ctx)]


def gather_blocks(block, n_ctx, me):
    held = block[None]
    for bit in reversed(range(ctx_bits(n_ctx))):
        other = lax.ppermute(held, "ctx", xor_pairs(n_ctx, bit))
        mine_first = ((me >> bit) & 1) == 0
        pair = jnp.where(
            mine_first, jnp.stack([held, other], axis=1), jnp.stack([other, held], axis=1)
        )
        held = pair.reshape((-1,) + block.shape)
    return held


def scatter_sum(blocks, n_ctx, me):
    acc = blocks
    for bit in range(ctx_bits(n_ctx)):
        halves = acc.reshape((-1, 2) + acc.shape[1:])
        keep_first = ((me >> bit) & 1) == 0
        keep = jnp.where(keep_first, halves[:, 0], halves[:, 1])
        send = jnp.where(keep_first, halves[:, 1], halves[:, 0]).astype(jnp.bfloat16)
        got = lax.ppermute(send, "ctx", xor_pairs(n_ctx, bit))
        acc = keep.astype(jnp.float32) + got.astype(jnp.float32)
    return acc[0]


def all_sum(values, n_ctx):
    for bit in range(ctx_bits(n_ctx)):
        values = values + lax.ppermute(values, "ctx", xor_pairs(n_ctx, bit))
    return values


def with_cols(rows, values, pad):
    hi, lo = split_f32(values)
    zeros = jnp.zeros((rows.shape[0], pad - 2), jnp.bfloat16)
    return jnp.concatenate([rows, hi[:, None], lo[:, None], zeros], axis=1)


def shards(tokens, cotangent, expert_ids, route_gates, w_gate, w_up, w_down):
    tok_rows, routes = expert_ids.shape
    experts = lax.axis_size("ep")
    n_ctx = lax.axis_size("ctx")
    me = lax.axis_index("ctx")
    capacity = 3 * tok_rows * routes // (2 * experts)
    slot_count = experts * capacity
    col_width = tokens.shape[1]
    pad = 128
    route_maps = route_onehot(expert_ids, experts, capacity)

    def place(values):
        placed = jnp.zeros((slot_count, values.shape[1]), jnp.float32)
        for chosen in route_maps:
            placed = placed + jnp.einsum(
                "ts,tc->sc", chosen.astype(jnp.bfloat16), values, preferred_element_type=jnp.float32
            )
        return placed.astype(jnp.bfloat16)

    def to_experts(rows):
        sent = rows.reshape(experts, capacity, rows.shape[1])
        got = lax.all_to_all(sent, "ep", split_axis=0, concat_axis=0, tiled=True)
        return got.reshape(slot_count, rows.shape[1])

    slot_gates = jnp.zeros((slot_count,), jnp.float32)
    for r, chosen in enumerate(route_maps):
        slot_gates = slot_gates + jnp.sum(jnp.where(chosen, route_gates[:, r][:, None], 0.0), axis=0)
    got_x = to_experts(with_cols(place(tokens), slot_gates, pad))
    gate_column = join_f32(got_x[:, col_width], got_x[:, col_width + 1])[:, None]
    rows_in = gather_blocks(got_x[:, :col_width], n_ctx, me)
    got_dy = to_experts(place(cotangent))
    grads_in = gather_blocks(got_dy, n_ctx, me)

    group = w_gate.shape[2]
    gate_w = w_gate[0].reshape(n_ctx, col_width, group)
    up_w = w_up[0].reshape(n_ctx, col_width, group)
    down_w = w_down[0]
    down_cols = [down_w[:, q * col_width : (q + 1) * col_width] for q in range(n_ctx)]

    pre_gate = jnp.einsum("nsd,ndf->sf", rows_in, gate_w, preferred_element_type=jnp.float32)
    pre_up = jnp.einsum("nsd,ndf->sf", rows_in, up_w, preferred_element_type=jnp.float32)
    sigma = jax.nn.sigmoid(pre_gate)
    activated = pre_gate * sigma
    hidden = (activated * pre_up).astype(jnp.bfloat16)
    partial_out = jnp.stack(
        [jnp.dot(hidden, cols, preferred_element_type=jnp.float32) for cols in down_cols]
    ).astype(jnp.bfloat16)
    gate_part = jnp.einsum(
        "nsd,nsd->s", partial_out.astype(jnp.float32), grads_in.astype(jnp.float32)
    )
    expert_out = scatter_sum(partial_out, n_ctx, me).astype(jnp.bfloat16)
    gate_sum = all_sum(gate_part, n_ctx)
    back_out = to_experts(with_cols(expert_out, gate_sum, pad))

    contract_last = (((1,), (1,)), ((), ()))
    down_t = sum(
        lax.dot_general(grads_in[q], down_cols[q], contract_last, preferred_element_type=jnp.float32)
        for q in range(n_ctx)
    )
    hidden_grad = gate_column * down_t
    grad_gate = (hidden_grad * pre_up * sigma * (1.0 + pre_gate * (1.0 - sigma))).astype(
        jnp.bfloat16
    )
    grad_up = (hidden_grad * activated).astype(jnp.bfloat16)
    back_terms = jnp.einsum(
        "sf,ndf->nsd", grad_gate, gate_w, preferred_element_type=jnp.float32
    ) + jnp.einsum("sf,ndf->nsd", grad_up, up_w, preferred_element_type=jnp.float32)
    back_terms = back_terms.astype(jnp.bfloat16)
    slot_grad = scatter_sum(back_terms, n_ctx, me).astype(jnp.bfloat16)
    back_grad = to_experts(slot_grad)

    w_gate_grad = jnp.einsum(
        "nsd,sf->ndf", rows_in, grad_gate, preferred_element_type=jnp.float32
    ).astype(jnp.bfloat16).reshape(1, n_ctx * col_width, group)
    w_up_grad = jnp.einsum(
        "nsd,sf->ndf", rows_in, grad_up, preferred_element_type=jnp.float32
    ).astype(jnp.bfloat16).reshape(1, n_ctx * col_width, group)

    layer_out = jnp.zeros((tok_rows, col_width), jnp.float32)
    input_grad = jnp.zeros((tok_rows, col_width), jnp.float32)
    gate_terms = []
    for r, chosen in enumerate(route_maps):
        pick = chosen.astype(jnp.bfloat16)
        rows_r = jnp.dot(pick, back_out, preferred_element_type=jnp.float32)
        layer_out = layer_out + route_gates[:, r][:, None] * rows_r[:, :col_width]
        input_grad = input_grad + jnp.dot(pick, back_grad, preferred_element_type=jnp.float32)
        gate_terms.append(rows_r[:, col_width] + rows_r[:, col_width + 1])
    gate_grad = jnp.stack(gate_terms, axis=1)
    return (
        layer_out.astype(jnp.bfloat16),
        input_grad.astype(jnp.bfloat16),
        gate_grad,
        w_gate_grad,
        w_up_grad,
    )


def solution(mesh):
    in_specs = (
        P("ep", "ctx"),
        P("ep", "ctx"),
        P("ep", None),
        P("ep", None),
        P("ep", None, "ctx"),
        P("ep", None, "ctx"),
        P("ep", "ctx", None),
    )
    out_specs = (
        P("ep", "ctx"),
        P("ep", "ctx"),
        P("ep", None),
        P("ep", None, "ctx"),
        P("ep", None, "ctx"),
    )
    return jax.shard_map(shards, mesh=mesh, in_specs=in_specs, out_specs=out_specs, check_vma=False)
```

```python
import jax
import jax.numpy as jnp
from jax import lax
from jax.sharding import PartitionSpec as P


def route_onehot(expert_ids, experts, capacity):
    tok_rows, routes = expert_ids.shape
    flat_ids = expert_ids.reshape(-1)
    labels = jnp.arange(experts, dtype=jnp.int32)
    onehot = (flat_ids[:, None] == labels[None, :]).astype(jnp.bfloat16)
    pairs = jnp.arange(flat_ids.shape[0], dtype=jnp.int32)
    before = (pairs[:, None] > pairs[None, :]).astype(jnp.bfloat16)
    earlier = jnp.dot(before, onehot, preferred_element_type=jnp.float32)
    slot_rank = jnp.sum(earlier * onehot.astype(jnp.float32), axis=1).astype(jnp.int32)
    slot_ids = (flat_ids * capacity + slot_rank).reshape(tok_rows, routes)
    positions = jnp.arange(experts * capacity, dtype=jnp.int32)
    return [slot_ids[:, r][:, None] == positions[None, :] for r in range(routes)]


def split_f32(values):
    hi = values.astype(jnp.bfloat16)
    lo = (values - hi.astype(jnp.float32)).astype(jnp.bfloat16)
    return hi, lo


def join_f32(hi, lo):
    return hi.astype(jnp.float32) + lo.astype(jnp.float32)


def ctx_bits(n_ctx):
    bits = n_ctx.bit_length() - 1
    assert 1 << bits == n_ctx
    return bits


def xor_pairs(n_ctx, bit):
    return [(i, i ^ (1 << bit)) for i in range(n_ctx)]


def gather_blocks(block, n_ctx, me):
    held = block[None]
    for bit in reversed(range(ctx_bits(n_ctx))):
        other = lax.ppermute(held, "ctx", xor_pairs(n_ctx, bit))
        mine_first = ((me >> bit) & 1) == 0
        pair = jnp.where(
            mine_first, jnp.stack([held, other], axis=1), jnp.stack([other, held], axis=1)
        )
        held = pair.reshape((-1,) + block.shape)
    return held


def scatter_sum(blocks, n_ctx, me):
    acc = blocks
    for bit in range(ctx_bits(n_ctx)):
        halves = acc.reshape((-1, 2) + acc.shape[1:])
        keep_first = ((me >> bit) & 1) == 0
        keep = jnp.where(keep_first, halves[:, 0], halves[:, 1])
        send = jnp.where(keep_first, halves[:, 1], halves[:, 0]).astype(jnp.bfloat16)
        got = lax.ppermute(send, "ctx", xor_pairs(n_ctx, bit))
        acc = keep + got.astype(jnp.float32)
    return acc[0]


def all_sum(values, n_ctx):
    for bit in range(ctx_bits(n_ctx)):
        values = values + lax.ppermute(values, "ctx", xor_pairs(n_ctx, bit))
    return values


def with_cols(rows, values, pad):
    hi, lo = split_f32(values)
    zeros = jnp.zeros((rows.shape[0], pad - 2), jnp.bfloat16)
    return jnp.concatenate([rows, hi[:, None], lo[:, None], zeros], axis=1)


def shards(tokens, cotangent, expert_ids, route_gates, w_gate, w_up, w_down):
    tok_rows, routes = expert_ids.shape
    experts = lax.axis_size("ep")
    n_ctx = lax.axis_size("ctx")
    me = lax.axis_index("ctx")
    capacity = 3 * tok_rows * routes // (2 * experts)
    slot_count = experts * capacity
    col_width = tokens.shape[1]
    pad = 128
    route_maps = route_onehot(expert_ids, experts, capacity)

    def place(values):
        placed = jnp.zeros((slot_count, values.shape[1]), jnp.float32)
        for chosen in route_maps:
            placed = placed + jnp.einsum(
                "ts,tc->sc", chosen.astype(jnp.bfloat16), values, preferred_element_type=jnp.float32
            )
        return placed.astype(jnp.bfloat16)

    def to_experts(rows):
        sent = rows.reshape(experts, capacity, rows.shape[1])
        got = lax.all_to_all(sent, "ep", split_axis=0, concat_axis=0, tiled=True)
        return got.reshape(slot_count, rows.shape[1])

    slot_gates = jnp.zeros((slot_count,), jnp.float32)
    for r, chosen in enumerate(route_maps):
        slot_gates = slot_gates + jnp.sum(jnp.where(chosen, route_gates[:, r][:, None], 0.0), axis=0)
    got_x = to_experts(with_cols(place(tokens), slot_gates, pad))
    gate_column = join_f32(got_x[:, col_width], got_x[:, col_width + 1])[:, None]
    rows_in = gather_blocks(got_x[:, :col_width], n_ctx, me)
    got_dy = to_experts(place(cotangent))
    grads_in = gather_blocks(got_dy, n_ctx, me)

    group = w_gate.shape[2]
    gate_w = w_gate[0].reshape(n_ctx, col_width, group)
    up_w = w_up[0].reshape(n_ctx, col_width, group)
    down_w = w_down[0]
    down_cols = [down_w[:, q * col_width : (q + 1) * col_width] for q in range(n_ctx)]

    pre_gate = jnp.einsum("nsd,ndf->sf", rows_in, gate_w, preferred_element_type=jnp.float32)
    pre_up = jnp.einsum("nsd,ndf->sf", rows_in, up_w, preferred_element_type=jnp.float32)
    sigma = jax.nn.sigmoid(pre_gate)
    activated = pre_gate * sigma
    hidden = (activated * pre_up).astype(jnp.bfloat16)
    partial_out = jnp.stack(
        [jnp.dot(hidden, cols, preferred_element_type=jnp.float32) for cols in down_cols]
    ).astype(jnp.bfloat16)
    gate_part = jnp.sum(
        partial_out.astype(jnp.float32) * grads_in.astype(jnp.float32), axis=(0, 2)
    )
    expert_out = scatter_sum(partial_out.astype(jnp.float32), n_ctx, me).astype(jnp.bfloat16)
    gate_sum = all_sum(gate_part, n_ctx)
    back_out = to_experts(with_cols(expert_out, gate_sum, pad))

    contract_last = (((1,), (1,)), ((), ()))
    down_t = sum(
        lax.dot_general(grads_in[q], down_cols[q], contract_last, preferred_element_type=jnp.float32)
        for q in range(n_ctx)
    )
    hidden_grad = gate_column * down_t
    grad_gate = (hidden_grad * pre_up * sigma * (1.0 + pre_gate * (1.0 - sigma))).astype(
        jnp.bfloat16
    )
    grad_up = (hidden_grad * activated).astype(jnp.bfloat16)
    back_terms = jnp.einsum(
        "sf,ndf->nsd", grad_gate, gate_w, preferred_element_type=jnp.float32
    ) + jnp.einsum("sf,ndf->nsd", grad_up, up_w, preferred_element_type=jnp.float32)
    back_terms = back_terms.astype(jnp.bfloat16).astype(jnp.float32)
    slot_grad = scatter_sum(back_terms, n_ctx, me).astype(jnp.bfloat16)
    back_grad = to_experts(slot_grad)

    w_gate_grad = jnp.einsum(
        "nsd,sf->ndf", rows_in, grad_gate, preferred_element_type=jnp.float32
    ).astype(jnp.bfloat16).reshape(1, n_ctx * col_width, group)
    w_up_grad = jnp.einsum(
        "nsd,sf->ndf", rows_in, grad_up, preferred_element_type=jnp.float32
    ).astype(jnp.bfloat16).reshape(1, n_ctx * col_width, group)

    layer_out = jnp.zeros((tok_rows, col_width), jnp.float32)
    input_grad = jnp.zeros((tok_rows, col_width), jnp.float32)
    gate_terms = []
    for r, chosen in enumerate(route_maps):
        pick = chosen.astype(jnp.bfloat16)
        rows_r = jnp.dot(pick, back_out, preferred_element_type=jnp.float32)
        layer_out = layer_out + route_gates[:, r][:, None] * rows_r[:, :col_width]
        input_grad = input_grad + jnp.dot(pick, back_grad, preferred_element_type=jnp.float32)
        gate_terms.append(rows_r[:, col_width] + rows_r[:, col_width + 1])
    gate_grad = jnp.stack(gate_terms, axis=1)
    return (
        layer_out.astype(jnp.bfloat16),
        input_grad.astype(jnp.bfloat16),
        gate_grad,
        w_gate_grad,
        w_up_grad,
    )


def solution(mesh):
    in_specs = (
        P("ep", "ctx"),
        P("ep", "ctx"),
        P("ep", None),
        P("ep", None),
        P("ep", None, "ctx"),
        P("ep", None, "ctx"),
        P("ep", "ctx", None),
    )
    out_specs = (
        P("ep", "ctx"),
        P("ep", "ctx"),
        P("ep", None),
        P("ep", None, "ctx"),
        P("ep", None, "ctx"),
    )
    return jax.shard_map(shards, mesh=mesh, in_specs=in_specs, out_specs=out_specs, check_vma=False)
```
